256 devices in a mesh: section: 8 (over x, core), blk: 32 (over y, z).
Axes of the slice: x: 4, y: 4, z: 8, core: 2. Of those that a mesh axis runs over, the one named last changes fastest.
Arguments:
- features: bfloat16 [4, 16384, 256], P(None, 'blk'), may hold values from -6 to 6
- tile_values: bfloat16 [4, 2560, 128, 128], P(None, 'blk'), may hold values from -1 to 1
- tile_rows: int32 [4, 2560], P(None, 'blk'), may hold values from 0 to 127, as said below
- tile_cols: int32 [4, 2560], P(None, 'blk'), may hold values from 0 to 127, as said below
- tile_count: int32 [4, 32], P(None, 'blk'), may hold values from 10 to 80, as said below
- degrees: int32 [4, 16384], P(None, 'blk'), may hold values from 16 to 64
- self_weight: bfloat16 [8, 256, 256], P('section'), may hold values from -0.375 to 0.375
- neighbour_weight: bfloat16 [8, 256, 256], P('section'), may hold values from -0.375 to 0.375
Outputs:
- layer_outputs: bfloat16 [8, 4, 16384, 256], P('section', None, 'blk')
The draws below stay inside these ranges and needn't reach their ends.
Inputs may be any that keep to these rules, and one draw needn't show every extreme that they name: `tile_rows`: slot k names a row block of its own blk index: between 4 * (k div 80) and 4 * (k div 80) + 3. `tile_cols`: slot k names a column block of a blk index at most 2 away from k div 80, counting around the axis; the 80 slots of one blk index name distinct row and column block pairs. `tile_count`: in every batch some blk index has all 80 slots live.
All inputs are finite; a program needn't handle non-finite values.
Results may differ from the reference program's by a relative error of at most 0.017.
Values may be sent and summed in bfloat16 or wider, within the bound.
No kernel may reach another device: no remote copies, remote signals or barrier semaphores. Data moves between devices by JAX's collectives and lax.ppermute only.
A program may use at most 64 MiB of HBM per device.

```python
import jax
import jax.numpy as jnp
from jax import lax

F = 256
BLOCK = 128
REACH = 2
NB_DEV = 4
BATCHES = 4
TMAX = 80
SLOTS = 2560
NBLOCKS = 128
NODES = 16384
LAYERS = 8
N_BLK = 32


def tile_layout(key):
    devices = NBLOCKS // NB_DEV
    band = (2 * REACH + 1) * NB_DEV
    scores = jax.random.randint(jax.random.fold_in(key, 11), (BATCHES, devices, TMAX), 0, 1 << 20)
    scores = scores * TMAX + jnp.arange(TMAX, dtype=jnp.int32)
    ordering = jnp.argsort(scores, axis=-1).astype(jnp.int32)
    local_row = ordering // band
    remainder = ordering % band
    offset = remainder // NB_DEV - REACH
    column_part = remainder % NB_DEV
    owners = jnp.arange(devices, dtype=jnp.int32)[None, :, None]
    rows = owners * NB_DEV + local_row
    cols = jnp.mod(owners + offset, devices) * NB_DEV + column_part
    return (rows.reshape(BATCHES, SLOTS).astype(jnp.int32), cols.reshape(BATCHES, SLOTS).astype(jnp.int32))


def draw_tile_rows(key, part):
    return tile_layout(key)[0]


def draw_tile_cols(key, part):
    return tile_layout(key)[1]


def draw_tile_count(key, part):
    devices = NBLOCKS // NB_DEV
    lowest = max(1, TMAX // 8)
    spread = TMAX - lowest
    first = jax.random.randint(jax.random.fold_in(key, 3), (BATCHES, devices), 0, spread + 1)
    second = jax.random.randint(jax.random.fold_in(key, 5), (BATCHES, devices), 0, spread + 1)
    counts = lowest + first * second // spread
    busiest = jax.random.randint(jax.random.fold_in(key, 9), (BATCHES, 1), 0, devices)
    counts = jnp.where(jnp.arange(devices, dtype=jnp.int32)[None, :] == busiest, TMAX, counts)
    return counts.astype(jnp.int32)


def place_ends(values, rng, least, high):
    extent = values.shape
    spot = [jax.random.randint(jax.random.fold_in(rng, axis), (), 0, extent[axis]) for axis in range(len(extent))]
    values = values.at[tuple(spot)].set(least)
    longest = extent.index(max(extent))
    spot[longest] = (spot[longest] + 1) % extent[longest]
    return values.at[tuple(spot)].set(high)


def block_levels(stream_key, extent, cuts, low, largest):
    def one(position, blocks):
        heights = jax.random.uniform(jax.random.fold_in(jax.random.fold_in(stream_key, 6), position), (blocks,), jnp.float32, low / len(cuts), largest / len(cuts))
        return jnp.repeat(jnp.exp(heights), extent[position] // blocks).reshape((-1,) + (1,) * (len(extent) - position - 1))

    gain = one(*cuts[0])
    for cut in cuts[1:]:
        gain = gain * one(*cut)
    return gain


def bell_draw(key, dims, deviation, reach, split=(), kind=jnp.bfloat16):
    values = deviation * jax.random.normal(key, dims, jnp.float32)
    if split:
        values = values * block_levels(key, dims, split, -0.22, 0.18)
    return jnp.clip(values, -reach, reach).astype(kind)


def setup_inputs(seed: int = 0) -> dict:
    seeds = jax.random.split(jax.random.key(seed), 9)
    return {
        "features": bell_draw(seeds[0], (BATCHES, NODES, F), 1.0, 6.0, ((1, 32),)),
        "tile_values": jnp.clip(jax.random.uniform(seeds[1], (BATCHES, SLOTS, BLOCK, BLOCK), jnp.float32, -1.0, 1.0) * block_levels(seeds[1], (BATCHES, SLOTS, BLOCK, BLOCK), ((1, 32),), -0.4, 0.0), -1.0, 1.0).astype(jnp.bfloat16),
        "tile_rows": draw_tile_rows(jax.random.fold_in(seeds[8], 71), 0),
        "tile_cols": draw_tile_cols(jax.random.fold_in(seeds[8], 71), 0),
        "tile_count": draw_tile_count(jax.random.fold_in(seeds[8], 71), 0),
        "degrees": place_ends(jax.random.randint(seeds[5], (BATCHES, NODES), 16, 65), jax.random.fold_in(seeds[5], 1), 16, 64).astype(jnp.int32),
        "self_weight": bell_draw(seeds[6], (LAYERS, F, F), F ** -0.5, 0.375, ((0, 8),)),
        "neighbour_weight": bell_draw(seeds[7], (LAYERS, F, F), F ** -0.5, 0.375, ((0, 8),)),
    }


def node_layer(hidden, values, rows, cols, count, degree, self_matrix, neighbour_matrix):
    blocks = hidden.reshape(NBLOCKS, BLOCK, F)

    def group_sum(group_args):
        group_values, group_rows, group_cols, group_count, owners = group_args
        gathered = blocks[group_cols].astype(jnp.float32)
        product = jnp.einsum('kij,kjf->kif', group_values.astype(jnp.float32), gathered)
        alive = jnp.arange(TMAX, dtype=jnp.int32) < group_count
        local_rows = group_rows - owners * NB_DEV
        select = ((local_rows[None, :] == jnp.arange(NB_DEV, dtype=jnp.int32)[:, None]) & alive[None, :]).astype(jnp.float32)
        return jnp.einsum('rk,kif->rif', select, product)
    sums = lax.map(group_sum, (values.reshape(N_BLK, TMAX, BLOCK, BLOCK), rows.reshape(N_BLK, TMAX), cols.reshape(N_BLK, TMAX), count, jnp.arange(N_BLK, dtype=jnp.int32)))
    summed = sums.reshape(NODES, F)
    neighbour_mean = (summed / degree.astype(jnp.float32)[:, None]).astype(jnp.bfloat16)
    combined = jnp.dot(hidden, self_matrix, preferred_element_type=jnp.float32) + jnp.dot(neighbour_mean, neighbour_matrix, preferred_element_type=jnp.float32)
    active = jnp.maximum(combined, 0.0)
    scale = lax.rsqrt(lax.optimization_barrier(jnp.mean(active * active, axis=-1, keepdims=True)) + 1e-05)
    return (active * scale).astype(jnp.bfloat16)

def reference(features, tile_values, tile_rows, tile_cols, tile_count, degrees, self_weight, neighbour_weight):
    results = []
    for batch in range(BATCHES):
        hidden = features[batch]
        per_layer = []
        for level in range(LAYERS):
            hidden = node_layer(hidden, tile_values[batch], tile_rows[batch], tile_cols[batch], tile_count[batch], degrees[batch], self_weight[level], neighbour_weight[level])
            per_layer.append(hidden)
        results.append(jnp.stack(per_layer))
    return jnp.stack(results, axis=1)
```

```python
import jax
import jax.numpy as jnp
from jax import lax
from jax.sharding import PartitionSpec as P

REACH = 2


def body(
    features, tile_values, tile_rows, tile_cols, tile_count, degrees, self_weight, neighbour_weight
):
    batch_total, rows_dev, feature_width = features.shape
    slot_total, block_size = tile_values.shape[1], tile_values.shape[2]
    blocks_dev = rows_dev // block_size
    window_span = 2 * REACH + 1
    band_width = window_span * blocks_dev
    blk_count = lax.axis_size("blk")
    section_count = lax.axis_size("section")
    layer_total = section_count
    blk_index = lax.axis_index("blk")
    section_index = lax.axis_index("section")

    self_all = lax.all_gather(self_weight[0], "section")
    neighbour_all = lax.all_gather(neighbour_weight[0], "section")

    group = section_count // batch_total
    workers = [group * m + group - 1 for m in range(batch_total)]
    batch = section_index // group

    def halo(x, by):
        pairs = []
        for s in workers:
            for b in range(blk_count):
                pairs.append((s * blk_count + b, s * blk_count + (b + by) % blk_count))
        return lax.ppermute(x, ("section", "blk"), pairs)

    values = lax.dynamic_index_in_dim(tile_values, batch, 0, keepdims=False)
    rows = lax.dynamic_index_in_dim(tile_rows, batch, 0, keepdims=False)
    cols = lax.dynamic_index_in_dim(tile_cols, batch, 0, keepdims=False)
    count = lax.dynamic_index_in_dim(tile_count, batch, 0, keepdims=False)[0]
    degree = lax.dynamic_index_in_dim(degrees, batch, 0, keepdims=False)
    hidden = lax.dynamic_index_in_dim(features, batch, 0, keepdims=False)

    column_dev = cols // blocks_dev
    shifted = jnp.mod(column_dev - blk_index + REACH, blk_count)
    column_local = shifted * blocks_dev + jnp.mod(cols, blocks_dev)
    row_local = rows - blk_index * blocks_dev
    alive = jnp.arange(slot_total, dtype=jnp.int32) < count
    target = row_local * band_width + column_local
    placing = (
        (target[None, :] == jnp.arange(blocks_dev * band_width, dtype=jnp.int32)[:, None])
        & alive[None, :]
    ).astype(jnp.bfloat16)
    slab = jnp.dot(
        placing,
        values.reshape(slot_total, block_size * block_size),
        preferred_element_type=jnp.float32,
    ).astype(jnp.bfloat16)
    band = (
        slab.reshape(blocks_dev, band_width, block_size, block_size)
        .transpose(0, 2, 1, 3)
        .reshape(rows_dev, window_span, rows_dev)
    )
    degree_f = degree.astype(jnp.float32)[:, None]

    outputs = []
    for level in range(layer_total):
        up1 = halo(hidden, 1)
        down1 = halo(hidden, -1)
        up2 = halo(up1, 1)
        down2 = halo(down1, -1)
        parts = [up2, up1, hidden, down1, down2]
        summed = jnp.dot(band[:, REACH, :], hidden, preferred_element_type=jnp.float32)
        for position in (REACH - 1, REACH + 1, REACH - 2, REACH + 2):
            summed = summed + jnp.dot(
                band[:, position, :], parts[position], preferred_element_type=jnp.float32
            )
        neighbour_mean = (summed / degree_f).astype(jnp.bfloat16)
        combined = jnp.dot(hidden, self_all[level], preferred_element_type=jnp.float32) + jnp.dot(
            neighbour_mean, neighbour_all[level], preferred_element_type=jnp.float32
        )
        active = jnp.maximum(combined, 0.0)
        scale = lax.rsqrt(jnp.mean(active * active, axis=-1, keepdims=True) + 1e-05)
        hidden = (active * scale).astype(jnp.bfloat16)
        outputs.append(hidden)

    gathered = []
    for m in range(batch_total):
        slot = jnp.zeros((rows_dev, feature_width), jnp.bfloat16)
        for level in range(layer_total):
            source = workers[m]
            if source == level:
                arrived = outputs[level]
            else:
                arrived = lax.ppermute(outputs[level], "section", [(source, level)])
            slot = jnp.where(section_index == level, arrived, slot)
        gathered.append(slot)
    return jnp.stack(gathered)[None]


def solution(mesh):
    return jax.shard_map(
        body,
        mesh=mesh,
        in_specs=(
            P(None, "blk", None),
            P(None, "blk", None, None),
            P(None, "blk"),
            P(None, "blk"),
            P(None, "blk"),
            P(None, "blk"),
            P("section", None, None),
            P("section", None, None),
        ),
        out_specs=P("section", None, "blk", None),
        check_vma=False,
    )
```

```python
import jax
import jax.numpy as jnp
from jax import lax
from jax.sharding import PartitionSpec as P

REACH = 2


def body(
    features, tile_values, tile_rows, tile_cols, tile_count, degrees, self_weight, neighbour_weight
):
    batch_total, rows_dev, feature_width = features.shape
    slot_total, block_size = tile_values.shape[1], tile_values.shape[2]
    blocks_dev = rows_dev // block_size
    window_span = 2 * REACH + 1
    band_width = window_span * blocks_dev
    blk_count = lax.axis_size("blk")
    section_count = lax.axis_size("section")
    layer_total = section_count
    blk_index = lax.axis_index("blk")
    section_index = lax.axis_index("section")

    weights_all = lax.all_gather(jnp.stack([self_weight[0], neighbour_weight[0]]), "section")
    self_all = weights_all[:, 0]
    neighbour_all = weights_all[:, 1]

    group = section_count // batch_total
    workers = [group * m + group - 1 for m in range(batch_total)]
    batch = section_index // group

    def halo(x, by):
        pairs = []
        for s in workers:
            for b in range(blk_count):
                pairs.append((s * blk_count + b, s * blk_count + (b + by) % blk_count))
        return lax.ppermute(x, ("section", "blk"), pairs)

    values = lax.dynamic_index_in_dim(tile_values, batch, 0, keepdims=False)
    rows = lax.dynamic_index_in_dim(tile_rows, batch, 0, keepdims=False)
    cols = lax.dynamic_index_in_dim(tile_cols, batch, 0, keepdims=False)
    count = lax.dynamic_index_in_dim(tile_count, batch, 0, keepdims=False)[0]
    degree = lax.dynamic_index_in_dim(degrees, batch, 0, keepdims=False)
    hidden = lax.dynamic_index_in_dim(features, batch, 0, keepdims=False)

    column_dev = cols // blocks_dev
    shifted = jnp.mod(column_dev - blk_index + REACH, blk_count)
    column_local = shifted * blocks_dev + jnp.mod(cols, blocks_dev)
    row_local = rows - blk_index * blocks_dev
    alive = jnp.arange(slot_total, dtype=jnp.int32) < count
    target = row_local * band_width + column_local
    placing = (
        (target[None, :] == jnp.arange(blocks_dev * band_width, dtype=jnp.int32)[:, None])
        & alive[None, :]
    ).astype(jnp.bfloat16)
    slab = jnp.dot(
        placing,
        values.reshape(slot_total, block_size * block_size),
        preferred_element_type=jnp.float32,
    ).astype(jnp.bfloat16)
    band = (
        slab.reshape(blocks_dev, band_width, block_size, block_size)
        .transpose(0, 2, 1, 3)
        .reshape(rows_dev, window_span, rows_dev)
    )
    degree_f = degree.astype(jnp.float32)[:, None]

    outputs = []
    for level in range(layer_total):
        up1 = halo(hidden, 1)
        down1 = halo(hidden, -1)
        up2 = halo(up1, 1)
        down2 = halo(down1, -1)
        parts = [up2, up1, hidden, down1, down2]
        summed = jnp.dot(band[:, REACH, :], hidden, preferred_element_type=jnp.float32)
        for position in (REACH - 1, REACH + 1, REACH - 2, REACH + 2):
            summed = summed + jnp.dot(
                band[:, position, :], parts[position], preferred_element_type=jnp.float32
            )
        neighbour_mean = (summed / degree_f).astype(jnp.bfloat16)
        combined = jnp.dot(hidden, self_all[level], preferred_element_type=jnp.float32) + jnp.dot(
            neighbour_mean, neighbour_all[level], preferred_element_type=jnp.float32
        )
        active = jnp.maximum(combined, 0.0)
        scale = lax.rsqrt(jnp.mean(active * active, axis=-1, keepdims=True) + 1e-05)
        hidden = (active * scale).astype(jnp.bfloat16)
        outputs.append(hidden)

    arrived = []
    for shift in range(section_count):
        candidates = [(w + shift) % section_count for w in workers]
        sending = outputs[candidates[0]]
        for w, level in zip(workers[1:], candidates[1:]):
            sending = jnp.where(section_index == w, outputs[level], sending)
        if shift == 0:
            arrived.append(sending)
        else:
            pairs = [(w, (w + shift) % section_count) for w in workers]
            arrived.append(lax.ppermute(sending, "section", pairs))
    arrived = jnp.stack(arrived)
    gathered = [
        lax.dynamic_index_in_dim(arrived, (section_index - w) % section_count, 0, keepdims=False)
        for w in workers
    ]
    return jnp.stack(gathered)[None]


def solution(mesh):
    return jax.shard_map(
        body,
        mesh=mesh,
        in_specs=(
            P(None, "blk", None),
            P(None, "blk", None, None),
            P(None, "blk"),
            P(None, "blk"),
            P(None, "blk"),
            P(None, "blk"),
            P("section", None, None),
            P("section", None, None),
        ),
        out_specs=P("section", None, "blk", None),
        check_vma=False,
    )
```

```python
import jax
import jax.numpy as jnp
from jax import lax
from jax.sharding import PartitionSpec as P

REACH = 2


def body(
    features, tile_values, tile_rows, tile_cols, tile_count, degrees, self_weight, neighbour_weight
):
    batch_total, rows_dev, feature_width = features.shape
    slot_total, block_size = tile_values.shape[1], tile_values.shape[2]
    blocks_dev = rows_dev // block_size
    window_span = 2 * REACH + 1
    band_width = window_span * blocks_dev
    blk_count = lax.axis_size("blk")
    section_count = lax.axis_size("section")
    layer_total = section_count
    blk_index = lax.axis_index("blk")
    section_index = lax.axis_index("section")

    weights_all = lax.all_gather(jnp.stack([self_weight[0], neighbour_weight[0]]), "section")
    self_all = weights_all[:, 0]
    neighbour_all = weights_all[:, 1]

    group = section_count // batch_total
    workers = [group * m + group - 1 for m in range(batch_total)]
    batch = section_index // group

    def halo(x, by):
        pairs = []
        for s in workers:
            for b in range(blk_count):
                pairs.append((s * blk_count + b, s * blk_count + (b + by) % blk_count))
        return lax.ppermute(x, ("section", "blk"), pairs)

    values = lax.dynamic_index_in_dim(tile_values, batch, 0, keepdims=False)
    rows = lax.dynamic_index_in_dim(tile_rows, batch, 0, keepdims=False)
    cols = lax.dynamic_index_in_dim(tile_cols, batch, 0, keepdims=False)
    count = lax.dynamic_index_in_dim(tile_count, batch, 0, keepdims=False)[0]
    degree = lax.dynamic_index_in_dim(degrees, batch, 0, keepdims=False)
    hidden = lax.dynamic_index_in_dim(features, batch, 0, keepdims=False)

    column_dev = cols // blocks_dev
    shifted = jnp.mod(column_dev - blk_index + REACH, blk_count)
    column_local = shifted * blocks_dev + jnp.mod(cols, blocks_dev)
    row_local = rows - blk_index * blocks_dev
    alive = jnp.arange(slot_total, dtype=jnp.int32) < count
    target = row_local * band_width + column_local
    placing = (
        (target[None, :] == jnp.arange(blocks_dev * band_width, dtype=jnp.int32)[:, None])
        & alive[None, :]
    ).astype(jnp.bfloat16)
    slab = jnp.dot(
        placing,
        values.reshape(slot_total, block_size * block_size),
        preferred_element_type=jnp.float32,
    ).astype(jnp.bfloat16)
    band = (
        slab.reshape(blocks_dev, band_width, block_size, block_size)
        .transpose(0, 2, 1, 3)
        .reshape(rows_dev, window_span, rows_dev)
    )
    degree_f = degree.astype(jnp.float32)[:, None]

    outputs = []
    for level in range(layer_total):
        up1 = halo(hidden, 1)
        down1 = halo(hidden, -1)
        up2 = halo(hidden, 2)
        down2 = halo(hidden, -2)
        parts = [up2, up1, hidden, down1, down2]
        summed = jnp.dot(band[:, REACH, :], hidden, preferred_element_type=jnp.float32)
        for position in (REACH - 1, REACH + 1, REACH - 2, REACH + 2):
            summed = summed + jnp.dot(
                band[:, position, :], parts[position], preferred_element_type=jnp.float32
            )
        neighbour_mean = (summed / degree_f).astype(jnp.bfloat16)
        combined = jnp.dot(hidden, self_all[level], preferred_element_type=jnp.float32) + jnp.dot(
            neighbour_mean, neighbour_all[level], preferred_element_type=jnp.float32
        )
        active = jnp.maximum(combined, 0.0)
        scale = lax.rsqrt(jnp.mean(active * active, axis=-1, keepdims=True) + 1e-05)
        hidden = (active * scale).astype(jnp.bfloat16)
        outputs.append(hidden)

    arrived = []
    for shift in range(section_count):
        candidates = [(w + shift) % section_count for w in workers]
        sending = outputs[candidates[0]]
        for w, level in zip(workers[1:], candidates[1:]):
            sending = jnp.where(section_index == w, outputs[level], sending)
        if shift == 0:
            arrived.append(sending)
        else:
            pairs = [(w, (w + shift) % section_count) for w in workers]
            arrived.append(lax.ppermute(sending, "section", pairs))
    arrived = jnp.stack(arrived)
    gathered = [
        lax.dynamic_index_in_dim(arrived, (section_index - w) % section_count, 0, keepdims=False)
        for w in workers
    ]
    return jnp.stack(gathered)[None]


def solution(mesh):
    return jax.shard_map(
        body,
        mesh=mesh,
        in_specs=(
            P(None, "blk", None),
            P(None, "blk", None, None),
            P(None, "blk"),
            P(None, "blk"),
            P(None, "blk"),
            P(None, "blk"),
            P("section", None, None),
            P("section", None, None),
        ),
        out_specs=P("section", None, "blk", None),
        check_vma=False,
    )
```

```python
import jax
import jax.numpy as jnp
from jax import lax
from jax.experimental import pallas as pl
from jax.experimental.pallas import tpu as pltpu
from jax.sharding import PartitionSpec as P

REACH = 2


def _band_kernel(rows_ref, cols_ref, count_ref, values_ref, band_ref):
    block = values_ref.shape[1]
    band_ref[...] = jnp.zeros(band_ref.shape, band_ref.dtype)

    def place(k, carry):
        r = pl.multiple_of(rows_ref[k] * block, block)
        c = pl.multiple_of(cols_ref[k] * block, block)
        band_ref[pl.ds(r, block), pl.ds(c, block)] = values_ref[k]
        return carry

    lax.fori_loop(0, count_ref[0], place, 0)


def build_band(row_local, column_local, count, values, rows_dev, band_cols):
    return pl.pallas_call(
        _band_kernel,
        out_shape=jax.ShapeDtypeStruct((rows_dev, band_cols), values.dtype),
        in_specs=[pl.BlockSpec(memory_space=pltpu.SMEM)] * 3
        + [pl.BlockSpec(memory_space=pltpu.VMEM)],
        out_specs=pl.BlockSpec(memory_space=pltpu.VMEM),
    )(row_local, column_local, count, values)


def _layer_kernel(band_ref, p0, p1, p2, p3, p4, degree_ref, ws_ref, wn_ref, out_ref):
    rows = p2.shape[0]
    parts = (p0, p1, p2, p3, p4)
    summed = jnp.dot(
        band_ref[:, pl.ds(2 * rows, rows)], p2[...], preferred_element_type=jnp.float32
    )
    for position in (1, 3, 0, 4):
        summed = summed + jnp.dot(
            band_ref[:, pl.ds(position * rows, rows)],
            parts[position][...],
            preferred_element_type=jnp.float32,
        )
    neighbour_mean = (summed / degree_ref[...]).astype(jnp.bfloat16)
    combined = jnp.dot(p2[...], ws_ref[...], preferred_element_type=jnp.float32) + jnp.dot(
        neighbour_mean, wn_ref[...], preferred_element_type=jnp.float32
    )
    active = jnp.maximum(combined, 0.0)
    scale = lax.rsqrt(jnp.mean(active * active, axis=-1, keepdims=True) + 1e-05)
    out_ref[...] = (active * scale).astype(out_ref.dtype)


def run_layer(band, parts, degree_f, ws, wn):
    rows, width = parts[2].shape
    return pl.pallas_call(
        _layer_kernel,
        out_shape=jax.ShapeDtypeStruct((rows, width), jnp.bfloat16),
        in_specs=[pl.BlockSpec(memory_space=pltpu.VMEM)] * 9,
        out_specs=pl.BlockSpec(memory_space=pltpu.VMEM),
        cost_estimate=pl.CostEstimate(
            flops=2 * rows * band.shape[1] * width + 4 * rows * width * width,
            bytes_accessed=band.size * 2 + 6 * rows * width * 2,
            transcendentals=rows,
        ),
    )(band, *parts, degree_f, ws, wn)


def body(
    features, tile_values, tile_rows, tile_cols, tile_count, degrees, self_weight, neighbour_weight
):
    batch_total, rows_dev, feature_width = features.shape
    slot_total, block_size = tile_values.shape[1], tile_values.shape[2]
    blocks_dev = rows_dev // block_size
    window_span = 2 * REACH + 1
    band_width = window_span * blocks_dev
    blk_count = lax.axis_size("blk")
    section_count = lax.axis_size("section")
    layer_total = section_count
    blk_index = lax.axis_index("blk")
    section_index = lax.axis_index("section")

    weights_all = lax.all_gather(jnp.stack([self_weight[0], neighbour_weight[0]]), "section")
    self_all = weights_all[:, 0]
    neighbour_all = weights_all[:, 1]

    group = section_count // batch_total
    workers = [group * m + group - 1 for m in range(batch_total)]
    batch = section_index // group

    def halo(x, by):
        pairs = []
        for s in workers:
            for b in range(blk_count):
                pairs.append((s * blk_count + b, s * blk_count + (b + by) % blk_count))
        return lax.ppermute(x, ("section", "blk"), pairs)

    values = lax.dynamic_index_in_dim(tile_values, batch, 0, keepdims=False)
    rows = lax.dynamic_index_in_dim(tile_rows, batch, 0, keepdims=False)
    cols = lax.dynamic_index_in_dim(tile_cols, batch, 0, keepdims=False)
    count = lax.dynamic_index_in_dim(tile_count, batch, 0, keepdims=False)[0]
    degree = lax.dynamic_index_in_dim(degrees, batch, 0, keepdims=False)
    hidden = lax.dynamic_index_in_dim(features, batch, 0, keepdims=False)

    column_dev = cols // blocks_dev
    shifted = jnp.mod(column_dev - blk_index + REACH, blk_count)
    column_local = shifted * blocks_dev + jnp.mod(cols, blocks_dev)
    row_local = rows - blk_index * blocks_dev
    band = build_band(
        jnp.clip(row_local, 0, blocks_dev - 1),
        jnp.clip(column_local, 0, band_width - 1),
        jnp.clip(count, 0, slot_total).reshape(1),
        values,
        rows_dev,
        band_width * block_size,
    )
    degree_f = degree.astype(jnp.float32)[:, None]

    outputs = []
    for level in range(layer_total):
        up1 = halo(hidden, 1)
        down1 = halo(hidden, -1)
        up2 = halo(up1, 1)
        down2 = halo(down1, -1)
        parts = [up2, up1, hidden, down1, down2]
        hidden = run_layer(band, parts, degree_f, self_all[level], neighbour_all[level])
        outputs.append(hidden)

    arrived = []
    for shift in range(section_count):
        candidates = [(w + shift) % section_count for w in workers]
        sending = outputs[candidates[0]]
        for w, level in zip(workers[1:], candidates[1:]):
            sending = jnp.where(section_index == w, outputs[level], sending)
        if shift == 0:
            arrived.append(sending)
        else:
            pairs = [(w, (w + shift) % section_count) for w in workers]
            arrived.append(lax.ppermute(sending, "section", pairs))
    arrived = jnp.stack(arrived)
    gathered = [
        lax.dynamic_index_in_dim(arrived, (section_index - w) % section_count, 0, keepdims=False)
        for w in workers
    ]
    return jnp.stack(gathered)[None]


def solution(mesh):
    return jax.shard_map(
        body,
        mesh=mesh,
        in_specs=(
            P(None, "blk", None),
            P(None, "blk", None, None),
            P(None, "blk"),
            P(None, "blk"),
            P(None, "blk"),
            P(None, "blk"),
            P("section", None, None),
            P("section", None, None),
        ),
        out_specs=P("section", None, "blk", None),
        check_vma=False,
    )
```

```python
import jax
import jax.numpy as jnp
from jax import lax
from jax.experimental import pallas as pl
from jax.experimental.pallas import tpu as pltpu
from jax.sharding import PartitionSpec as P

REACH = 2


def _band_kernel(rows_ref, cols_ref, count_ref, values_ref, band_ref):
    block = values_ref.shape[1]
    band_ref[...] = jnp.zeros(band_ref.shape, band_ref.dtype)

    def place(k, carry):
        r = pl.multiple_of(rows_ref[k] * block, block)
        c = pl.multiple_of(cols_ref[k] * block, block)
        band_ref[pl.ds(r, block), pl.ds(c, block)] = values_ref[k]
        return carry

    lax.fori_loop(0, count_ref[0], place, 0)


def build_band(row_local, column_local, count, values, rows_dev, band_cols):
    return pl.pallas_call(
        _band_kernel,
        out_shape=jax.ShapeDtypeStruct((rows_dev, band_cols), values.dtype),
        in_specs=[pl.BlockSpec(memory_space=pltpu.SMEM)] * 3
        + [pl.BlockSpec(memory_space=pltpu.VMEM)],
        out_specs=pl.BlockSpec(memory_space=pltpu.VMEM),
    )(row_local, column_local, count, values)


def _layer_kernel(band_ref, p0, p1, p2, p3, p4, degree_ref, ws_ref, wn_ref, out_ref):
    rows = p2.shape[0]
    parts = (p0, p1, p2, p3, p4)
    summed = jnp.dot(
        band_ref[:, pl.ds(2 * rows, rows)], p2[...], preferred_element_type=jnp.float32
    )
    for position in (1, 3, 0, 4):
        summed = summed + jnp.dot(
            band_ref[:, pl.ds(position * rows, rows)],
            parts[position][...],
            preferred_element_type=jnp.float32,
        )
    neighbour_mean = (summed / degree_ref[...]).astype(jnp.bfloat16)
    combined = jnp.dot(p2[...], ws_ref[...], preferred_element_type=jnp.float32) + jnp.dot(
        neighbour_mean, wn_ref[...], preferred_element_type=jnp.float32
    )
    active = jnp.maximum(combined, 0.0)
    scale = lax.rsqrt(jnp.mean(active * active, axis=-1, keepdims=True) + 1e-05)
    out_ref[...] = (active * scale).astype(out_ref.dtype)


def run_layer(band, parts, degree_f, ws, wn):
    rows, width = parts[2].shape
    return pl.pallas_call(
        _layer_kernel,
        out_shape=jax.ShapeDtypeStruct((rows, width), jnp.bfloat16),
        in_specs=[pl.BlockSpec(memory_space=pltpu.VMEM)] * 9,
        out_specs=pl.BlockSpec(memory_space=pltpu.VMEM),
        cost_estimate=pl.CostEstimate(
            flops=2 * rows * band.shape[1] * width + 4 * rows * width * width,
            bytes_accessed=band.size * 2 + 6 * rows * width * 2,
            transcendentals=rows,
        ),
    )(band, *parts, degree_f, ws, wn)


def body(
    features, tile_values, tile_rows, tile_cols, tile_count, degrees, self_weight, neighbour_weight
):
    batch_total, rows_dev, feature_width = features.shape
    slot_total, block_size = tile_values.shape[1], tile_values.shape[2]
    blocks_dev = rows_dev // block_size
    window_span = 2 * REACH + 1
    band_width = window_span * blocks_dev
    blk_count = lax.axis_size("blk")
    section_count = lax.axis_size("section")
    layer_total = section_count
    blk_index = lax.axis_index("blk")
    section_index = lax.axis_index("section")

    weights_all = lax.all_gather(jnp.stack([self_weight[0], neighbour_weight[0]]), "section")
    self_all = weights_all[:, 0]
    neighbour_all = weights_all[:, 1]

    group = section_count // batch_total
    batch = section_index // group
    odd = section_index % 2 == 1

    def halo(x, reach):
        pairs = []
        for s in range(section_count):
            by = reach if s % 2 == 1 else -reach
            for b in range(blk_count):
                pairs.append((s * blk_count + b, s * blk_count + (b + by) % blk_count))
        return lax.ppermute(x, ("section", "blk"), pairs)

    def swap(x):
        pairs = [(s, s ^ 1) for s in range(section_count)]
        return lax.ppermute(x, "section", pairs)

    values = lax.dynamic_index_in_dim(tile_values, batch, 0, keepdims=False)
    rows = lax.dynamic_index_in_dim(tile_rows, batch, 0, keepdims=False)
    cols = lax.dynamic_index_in_dim(tile_cols, batch, 0, keepdims=False)
    count = lax.dynamic_index_in_dim(tile_count, batch, 0, keepdims=False)[0]
    degree = lax.dynamic_index_in_dim(degrees, batch, 0, keepdims=False)
    hidden = lax.dynamic_index_in_dim(features, batch, 0, keepdims=False)

    column_dev = cols // blocks_dev
    shifted = jnp.mod(column_dev - blk_index + REACH, blk_count)
    shifted = jnp.where(odd, shifted, 2 * REACH - shifted)
    column_local = shifted * blocks_dev + jnp.mod(cols, blocks_dev)
    row_local = rows - blk_index * blocks_dev
    band = build_band(
        jnp.clip(row_local, 0, blocks_dev - 1),
        jnp.clip(column_local, 0, band_width - 1),
        jnp.clip(count, 0, slot_total).reshape(1),
        values,
        rows_dev,
        band_width * block_size,
    )
    degree_f = degree.astype(jnp.float32)[:, None]

    outputs = []
    for level in range(layer_total):
        near = halo(hidden, 1)
        far = halo(hidden, 2)
        theirs = swap(jnp.concatenate([near, far], axis=0))
        parts = [far, near, hidden, theirs[:rows_dev], theirs[rows_dev:]]
        hidden = run_layer(band, parts, degree_f, self_all[level], neighbour_all[level])
        outputs.append(hidden)

    stacked = jnp.stack(outputs)
    arrived = []
    for shift in range(0, section_count, group):
        sending = lax.dynamic_index_in_dim(
            stacked, (section_index + shift) % section_count, 0, keepdims=False
        )
        if shift == 0:
            arrived.append(sending)
        else:
            pairs = [(s, (s + shift) % section_count) for s in range(section_count)]
            arrived.append(lax.ppermute(sending, "section", pairs))
    arrived = jnp.stack(arrived)
    chip = section_index // group
    gathered = [
        lax.dynamic_index_in_dim(arrived, (chip - m) % batch_total, 0, keepdims=False)
        for m in range(batch_total)
    ]
    return jnp.stack(gathered)[None]


def solution(mesh):
    return jax.shard_map(
        body,
        mesh=mesh,
        in_specs=(
            P(None, "blk", None),
            P(None, "blk", None, None),
            P(None, "blk"),
            P(None, "blk"),
            P(None, "blk"),
            P(None, "blk"),
            P("section", None, None),
            P("section", None, None),
        ),
        out_specs=P("section", None, "blk", None),
        check_vma=False,
    )
```

```python
import jax
import jax.numpy as jnp
from jax import lax
from jax.experimental import pallas as pl
from jax.experimental.pallas import tpu as pltpu
from jax.sharding import PartitionSpec as P

REACH = 2


def _band_kernel(rows_ref, cols_ref, count_ref, values_ref, band_ref):
    block = values_ref.shape[1]
    band_ref[...] = jnp.zeros(band_ref.shape, band_ref.dtype)

    def place(k, carry):
        r = pl.multiple_of(rows_ref[k] * block, block)
        c = pl.multiple_of(cols_ref[k] * block, block)
        band_ref[pl.ds(r, block), pl.ds(c, block)] = values_ref[k]
        return carry

    lax.fori_loop(0, count_ref[0], place, 0)


def build_band(row_local, column_local, count, values, rows_dev, band_cols):
    return pl.pallas_call(
        _band_kernel,
        out_shape=jax.ShapeDtypeStruct((rows_dev, band_cols), values.dtype),
        in_specs=[pl.BlockSpec(memory_space=pltpu.SMEM)] * 3
        + [pl.BlockSpec(memory_space=pltpu.VMEM)],
        out_specs=pl.BlockSpec(memory_space=pltpu.VMEM),
    )(row_local, column_local, count, values)


def _own_kernel(band_ref, hidden_ref, rows_ref, ws_ref, summed_ref, self_ref):
    summed_ref[...] = jnp.dot(band_ref[...], hidden_ref[...], preferred_element_type=jnp.float32)
    self_ref[...] = jnp.dot(rows_ref[...], ws_ref[...], preferred_element_type=jnp.float32)


def own_part(band, hidden, ws, tile):
    rows, width = hidden.shape
    own = REACH
    f32 = jax.ShapeDtypeStruct((rows, width), jnp.float32)
    return pl.pallas_call(
        _own_kernel,
        out_shape=(f32, f32),
        grid=(rows // tile,),
        in_specs=[
            pl.BlockSpec((tile, rows), lambda i: (i, own)),
            pl.BlockSpec((rows, width), lambda i: (0, 0)),
            pl.BlockSpec((tile, width), lambda i: (i, 0)),
            pl.BlockSpec((width, width), lambda i: (0, 0)),
        ],
        out_specs=[
            pl.BlockSpec((tile, width), lambda i: (i, 0)),
            pl.BlockSpec((tile, width), lambda i: (i, 0)),
        ],
        cost_estimate=pl.CostEstimate(
            flops=2 * rows * rows * width + 2 * rows * width * width,
            bytes_accessed=rows * rows * 2 + 2 * rows * width * 2 + 2 * rows * width * 4,
            transcendentals=0,
        ),
    )(band, hidden, hidden, ws)


def _layer_kernel(band_ref, p0, p1, p3, p4, own_ref, self_ref, degree_ref, wn_ref, out_ref):
    rows = p0.shape[0]
    parts = {0: p0, 1: p1, 3: p3, 4: p4}
    summed = own_ref[...]
    for position in (1, 3, 0, 4):
        summed = summed + jnp.dot(
            band_ref[:, pl.ds(position * rows, rows)],
            parts[position][...],
            preferred_element_type=jnp.float32,
        )
    neighbour_mean = (summed / degree_ref[...]).astype(jnp.bfloat16)
    combined = self_ref[...] + jnp.dot(
        neighbour_mean, wn_ref[...], preferred_element_type=jnp.float32
    )
    active = jnp.maximum(combined, 0.0)
    scale = lax.rsqrt(jnp.mean(active * active, axis=-1, keepdims=True) + 1e-05)
    out_ref[...] = (active * scale).astype(out_ref.dtype)


def run_layer(band, parts, own, own_self, degree_f, wn, tile):
    rows, width = parts[2].shape
    band_cols = band.shape[1]
    whole = pl.BlockSpec((rows, width), lambda i: (0, 0))
    row_tile = pl.BlockSpec((tile, width), lambda i: (i, 0))
    return pl.pallas_call(
        _layer_kernel,
        out_shape=jax.ShapeDtypeStruct((rows, width), jnp.bfloat16),
        grid=(rows // tile,),
        in_specs=[
            pl.BlockSpec((tile, band_cols), lambda i: (i, 0)),
            whole,
            whole,
            whole,
            whole,
            row_tile,
            row_tile,
            pl.BlockSpec((tile, 1), lambda i: (i, 0)),
            pl.BlockSpec((width, width), lambda i: (0, 0)),
        ],
        out_specs=row_tile,
        cost_estimate=pl.CostEstimate(
            flops=2 * rows * (band_cols - rows) * width + 2 * rows * width * width,
            bytes_accessed=rows * band_cols * 2 + 6 * rows * width * 2 + 2 * rows * width * 4,
            transcendentals=rows,
        ),
    )(band, parts[0], parts[1], parts[3], parts[4], own, own_self, degree_f, wn)


def body(
    features, tile_values, tile_rows, tile_cols, tile_count, degrees, self_weight, neighbour_weight
):
    batch_total, rows_dev, feature_width = features.shape
    slot_total, block_size = tile_values.shape[1], tile_values.shape[2]
    blocks_dev = rows_dev // block_size
    window_span = 2 * REACH + 1
    band_width = window_span * blocks_dev
    blk_count = lax.axis_size("blk")
    section_count = lax.axis_size("section")
    layer_total = section_count
    blk_index = lax.axis_index("blk")
    section_index = lax.axis_index("section")

    weights_all = lax.all_gather(jnp.stack([self_weight[0], neighbour_weight[0]]), "section")
    self_all = weights_all[:, 0]
    neighbour_all = weights_all[:, 1]

    group = section_count // batch_total
    batch = section_index // group
    odd = section_index % 2 == 1

    def halo(x, reach):
        pairs = []
        for s in range(section_count):
            by = reach if s % 2 == 1 else -reach
            for b in range(blk_count):
                pairs.append((s * blk_count + b, s * blk_count + (b + by) % blk_count))
        return lax.ppermute(x, ("section", "blk"), pairs)

    def swap(x):
        pairs = [(s, s ^ 1) for s in range(section_count)]
        return lax.ppermute(x, "section", pairs)

    values = lax.dynamic_index_in_dim(tile_values, batch, 0, keepdims=False)
    rows = lax.dynamic_index_in_dim(tile_rows, batch, 0, keepdims=False)
    cols = lax.dynamic_index_in_dim(tile_cols, batch, 0, keepdims=False)
    count = lax.dynamic_index_in_dim(tile_count, batch, 0, keepdims=False)[0]
    degree = lax.dynamic_index_in_dim(degrees, batch, 0, keepdims=False)
    hidden = lax.dynamic_index_in_dim(features, batch, 0, keepdims=False)

    column_dev = cols // blocks_dev
    shifted = jnp.mod(column_dev - blk_index + REACH, blk_count)
    shifted = jnp.where(odd, shifted, 2 * REACH - shifted)
    column_local = shifted * blocks_dev + jnp.mod(cols, blocks_dev)
    row_local = rows - blk_index * blocks_dev
    band = build_band(
        jnp.clip(row_local, 0, blocks_dev - 1),
        jnp.clip(column_local, 0, band_width - 1),
        jnp.clip(count, 0, slot_total).reshape(1),
        values,
        rows_dev,
        band_width * block_size,
    )
    degree_f = degree.astype(jnp.float32)[:, None]

    outputs = []
    for level in range(layer_total):
        near = halo(hidden, 1)
        far = halo(hidden, 2)
        own, own_self = own_part(band, hidden, self_all[level], block_size)
        parts = [far, near, hidden, swap(near), swap(far)]
        hidden = run_layer(band, parts, own, own_self, degree_f, neighbour_all[level], block_size)
        outputs.append(hidden)

    stacked = jnp.stack(outputs)
    arrived = []
    for shift in range(0, section_count, group):
        sending = lax.dynamic_index_in_dim(
            stacked, (section_index + shift) % section_count, 0, keepdims=False
        )
        if shift == 0:
            arrived.append(sending)
        else:
            pairs = [(s, (s + shift) % section_count) for s in range(section_count)]
            arrived.append(lax.ppermute(sending, "section", pairs))
    arrived = jnp.stack(arrived)
    chip = section_index // group
    gathered = [
        lax.dynamic_index_in_dim(arrived, (chip - m) % batch_total, 0, keepdims=False)
        for m in range(batch_total)
    ]
    return jnp.stack(gathered)[None]


def solution(mesh):
    return jax.shard_map(
        body,
        mesh=mesh,
        in_specs=(
            P(None, "blk", None),
            P(None, "blk", None, None),
            P(None, "blk"),
            P(None, "blk"),
            P(None, "blk"),
            P(None, "blk"),
            P("section", None, None),
            P("section", None, None),
        ),
        out_specs=P("section", None, "blk", None),
        check_vma=False,
    )
```

```python
import jax
import jax.numpy as jnp
from jax import lax
from jax.experimental import pallas as pl
from jax.experimental.pallas import tpu as pltpu
from jax.sharding import PartitionSpec as P

REACH = 2


def _band_kernel(rows_ref, cols_ref, count_ref, values_ref, band_ref):
    block = values_ref.shape[1]
    band_ref[...] = jnp.zeros(band_ref.shape, band_ref.dtype)

    def place(k, carry):
        r = pl.multiple_of(rows_ref[k] * block, block)
        c = pl.multiple_of(cols_ref[k] * block, block)
        band_ref[pl.ds(r, block), pl.ds(c, block)] = values_ref[k]
        return carry

    lax.fori_loop(0, count_ref[0], place, 0)


def build_band(row_local, column_local, count, values, rows_dev, band_cols):
    return pl.pallas_call(
        _band_kernel,
        out_shape=jax.ShapeDtypeStruct((rows_dev, band_cols), values.dtype),
        in_specs=[pl.BlockSpec(memory_space=pltpu.SMEM)] * 3
        + [pl.BlockSpec(memory_space=pltpu.VMEM)],
        out_specs=pl.BlockSpec(memory_space=pltpu.VMEM),
    )(row_local, column_local, count, values)


def _layer_kernel(band_ref, p0, p1, p2, p3, p4, degree_ref, ws_ref, wn_ref, out_ref):
    rows = p2.shape[0]
    parts = (p0, p1, p2, p3, p4)
    summed = jnp.dot(
        band_ref[:, pl.ds(2 * rows, rows)], p2[...], preferred_element_type=jnp.float32
    )
    for position in (1, 3, 0, 4):
        summed = summed + jnp.dot(
            band_ref[:, pl.ds(position * rows, rows)],
            parts[position][...],
            preferred_element_type=jnp.float32,
        )
    neighbour_mean = (summed / degree_ref[...]).astype(jnp.bfloat16)
    combined = jnp.dot(p2[...], ws_ref[...], preferred_element_type=jnp.float32) + jnp.dot(
        neighbour_mean, wn_ref[...], preferred_element_type=jnp.float32
    )
    active = jnp.maximum(combined, 0.0)
    scale = lax.rsqrt(jnp.mean(active * active, axis=-1, keepdims=True) + 1e-05)
    out_ref[...] = (active * scale).astype(out_ref.dtype)


def run_layer(band, parts, degree_f, ws, wn):
    rows, width = parts[2].shape
    return pl.pallas_call(
        _layer_kernel,
        out_shape=jax.ShapeDtypeStruct((rows, width), jnp.bfloat16),
        in_specs=[pl.BlockSpec(memory_space=pltpu.VMEM)] * 9,
        out_specs=pl.BlockSpec(memory_space=pltpu.VMEM),
        cost_estimate=pl.CostEstimate(
            flops=2 * rows * band.shape[1] * width + 4 * rows * width * width,
            bytes_accessed=band.size * 2 + 6 * rows * width * 2,
            transcendentals=rows,
        ),
    )(band, *parts, degree_f, ws, wn)


def body(
    features, tile_values, tile_rows, tile_cols, tile_count, degrees, self_weight, neighbour_weight
):
    batch_total, rows_dev, feature_width = features.shape
    slot_total, block_size = tile_values.shape[1], tile_values.shape[2]
    blocks_dev = rows_dev // block_size
    window_span = 2 * REACH + 1
    band_width = window_span * blocks_dev
    blk_count = lax.axis_size("blk")
    section_count = lax.axis_size("section")
    layer_total = section_count
    blk_index = lax.axis_index("blk")
    section_index = lax.axis_index("section")

    weights_all = lax.all_gather(jnp.stack([self_weight[0], neighbour_weight[0]]), "section")
    self_all = weights_all[:, 0]
    neighbour_all = weights_all[:, 1]

    group = section_count // batch_total
    batch = section_index // group
    odd = section_index % 2 == 1

    def halo(x, reach):
        pairs = []
        for s in range(section_count):
            by = reach if s % 2 == 1 else -reach
            for b in range(blk_count):
                pairs.append((s * blk_count + b, s * blk_count + (b + by) % blk_count))
        return lax.ppermute(x, ("section", "blk"), pairs)

    def swap(x):
        pairs = [(s, s ^ 1) for s in range(section_count)]
        return lax.ppermute(x, "section", pairs)

    values = lax.dynamic_index_in_dim(tile_values, batch, 0, keepdims=False)
    rows = lax.dynamic_index_in_dim(tile_rows, batch, 0, keepdims=False)
    cols = lax.dynamic_index_in_dim(tile_cols, batch, 0, keepdims=False)
    count = lax.dynamic_index_in_dim(tile_count, batch, 0, keepdims=False)[0]
    degree = lax.dynamic_index_in_dim(degrees, batch, 0, keepdims=False)
    hidden = lax.dynamic_index_in_dim(features, batch, 0, keepdims=False)

    column_dev = cols // blocks_dev
    shifted = jnp.mod(column_dev - blk_index + REACH, blk_count)
    shifted = jnp.where(odd, shifted, 2 * REACH - shifted)
    column_local = shifted * blocks_dev + jnp.mod(cols, blocks_dev)
    row_local = rows - blk_index * blocks_dev
    band = build_band(
        jnp.clip(row_local, 0, blocks_dev - 1),
        jnp.clip(column_local, 0, band_width - 1),
        jnp.clip(count, 0, slot_total).reshape(1),
        values,
        rows_dev,
        band_width * block_size,
    )
    degree_f = degree.astype(jnp.float32)[:, None]

    outputs = []
    for level in range(layer_total):
        near = halo(hidden, 1)
        far = halo(hidden, 2)
        parts = [far, near, hidden, swap(near), swap(far)]
        hidden = run_layer(band, parts, degree_f, self_all[level], neighbour_all[level])
        outputs.append(hidden)

    stacked = jnp.stack(outputs)
    arrived = []
    for shift in range(0, section_count, group):
        sending = lax.dynamic_index_in_dim(
            stacked, (section_index + shift) % section_count, 0, keepdims=False
        )
        if shift == 0:
            arrived.append(sending)
        else:
            pairs = [(s, (s + shift) % section_count) for s in range(section_count)]
            arrived.append(lax.ppermute(sending, "section", pairs))
    arrived = jnp.stack(arrived)
    chip = section_index // group
    gathered = [
        lax.dynamic_index_in_dim(arrived, (chip - m) % batch_total, 0, keepdims=False)
        for m in range(batch_total)
    ]
    return jnp.stack(gathered)[None]


def solution(mesh):
    return jax.shard_map(
        body,
        mesh=mesh,
        in_specs=(
            P(None, "blk", None),
            P(None, "blk", None, None),
            P(None, "blk"),
            P(None, "blk"),
            P(None, "blk"),
            P(None, "blk"),
            P("section", None, None),
            P("section", None, None),
        ),
        out_specs=P("section", None, "blk", None),
        check_vma=False,
    )
```

```python
import jax
import jax.numpy as jnp
from jax import lax
from jax.experimental import pallas as pl
from jax.experimental.pallas import tpu as pltpu
from jax.sharding import PartitionSpec as P

REACH = 2


def _band_kernel(rows_ref, cols_ref, count_ref, values_ref, band_ref):
    block = values_ref.shape[1]
    band_ref[...] = jnp.zeros(band_ref.shape, band_ref.dtype)

    def place(k, carry):
        r = pl.multiple_of(rows_ref[k] * block, block)
        c = pl.multiple_of(cols_ref[k] * block, block)
        band_ref[pl.ds(r, block), pl.ds(c, block)] = values_ref[k]
        return carry

    lax.fori_loop(0, count_ref[0], place, 0)


def build_band(row_local, column_local, count, values, rows_dev, band_cols):
    return pl.pallas_call(
        _band_kernel,
        out_shape=jax.ShapeDtypeStruct((rows_dev, band_cols), values.dtype),
        in_specs=[pl.BlockSpec(memory_space=pltpu.SMEM)] * 3
        + [pl.BlockSpec(memory_space=pltpu.VMEM)],
        out_specs=pl.BlockSpec(memory_space=pltpu.VMEM),
    )(row_local, column_local, count, values)


def _layer_kernel(band_ref, p0, p1, p2, p3, p4, own_ref, degree_ref, ws_ref, wn_ref, out_ref):
    rows = p2.shape[0]
    parts = (p0, p1, p2, p3, p4)
    summed = jnp.dot(
        band_ref[:, pl.ds(2 * rows, rows)], p2[...], preferred_element_type=jnp.float32
    )
    for position in (1, 3, 0, 4):
        summed = summed + jnp.dot(
            band_ref[:, pl.ds(position * rows, rows)],
            parts[position][...],
            preferred_element_type=jnp.float32,
        )
    neighbour_mean = (summed / degree_ref[...]).astype(jnp.bfloat16)
    combined = jnp.dot(own_ref[...], ws_ref[...], preferred_element_type=jnp.float32) + jnp.dot(
        neighbour_mean, wn_ref[...], preferred_element_type=jnp.float32
    )
    active = jnp.maximum(combined, 0.0)
    scale = lax.rsqrt(jnp.mean(active * active, axis=-1, keepdims=True) + 1e-05)
    out_ref[...] = (active * scale).astype(out_ref.dtype)


def run_layer(band, parts, degree_f, weights_all, level, tile):
    rows, width = parts[2].shape
    band_cols = band.shape[1]
    whole = pl.BlockSpec((rows, width), lambda i: (0, 0))
    return pl.pallas_call(
        _layer_kernel,
        out_shape=jax.ShapeDtypeStruct((rows, width), jnp.bfloat16),
        grid=(rows // tile,),
        in_specs=[
            pl.BlockSpec((tile, band_cols), lambda i: (i, 0)),
            whole,
            whole,
            whole,
            whole,
            whole,
            pl.BlockSpec((tile, width), lambda i: (i, 0)),
            pl.BlockSpec((tile, 1), lambda i: (i, 0)),
            pl.BlockSpec((None, None, width, width), lambda i: (level, 0, 0, 0)),
            pl.BlockSpec((None, None, width, width), lambda i: (level, 1, 0, 0)),
        ],
        out_specs=pl.BlockSpec((tile, width), lambda i: (i, 0)),
        cost_estimate=pl.CostEstimate(
            flops=2 * rows * band_cols * width + 4 * rows * width * width,
            bytes_accessed=band.size * 2 + 6 * rows * width * 2,
            transcendentals=rows,
        ),
    )(band, *parts, parts[2], degree_f, weights_all, weights_all)


def body(
    features, tile_values, tile_rows, tile_cols, tile_count, degrees, self_weight, neighbour_weight
):
    batch_total, rows_dev, feature_width = features.shape
    slot_total, block_size = tile_values.shape[1], tile_values.shape[2]
    blocks_dev = rows_dev // block_size
    window_span = 2 * REACH + 1
    band_width = window_span * blocks_dev
    blk_count = lax.axis_size("blk")
    section_count = lax.axis_size("section")
    layer_total = section_count
    blk_index = lax.axis_index("blk")
    section_index = lax.axis_index("section")

    weights_all = lax.all_gather(jnp.stack([self_weight[0], neighbour_weight[0]]), "section")

    group = section_count // batch_total
    batch = section_index // group
    odd = section_index % 2 == 1

    def halo(x, reach):
        pairs = []
        for s in range(section_count):
            by = reach if s % 2 == 1 else -reach
            for b in range(blk_count):
                pairs.append((s * blk_count + b, s * blk_count + (b + by) % blk_count))
        return lax.ppermute(x, ("section", "blk"), pairs)

    def swap(x):
        pairs = [(s, s ^ 1) for s in range(section_count)]
        return lax.ppermute(x, "section", pairs)

    values = lax.dynamic_index_in_dim(tile_values, batch, 0, keepdims=False)
    rows = lax.dynamic_index_in_dim(tile_rows, batch, 0, keepdims=False)
    cols = lax.dynamic_index_in_dim(tile_cols, batch, 0, keepdims=False)
    count = lax.dynamic_index_in_dim(tile_count, batch, 0, keepdims=False)[0]
    degree = lax.dynamic_index_in_dim(degrees, batch, 0, keepdims=False)
    hidden = lax.dynamic_index_in_dim(features, batch, 0, keepdims=False)

    column_dev = cols // blocks_dev
    shifted = jnp.mod(column_dev - blk_index + REACH, blk_count)
    shifted = jnp.where(odd, shifted, 2 * REACH - shifted)
    column_local = shifted * blocks_dev + jnp.mod(cols, blocks_dev)
    row_local = rows - blk_index * blocks_dev
    band = build_band(
        jnp.clip(row_local, 0, blocks_dev - 1),
        jnp.clip(column_local, 0, band_width - 1),
        jnp.clip(count, 0, slot_total).reshape(1),
        values,
        rows_dev,
        band_width * block_size,
    )
    degree_f = degree.astype(jnp.float32)[:, None]

    outputs = []
    for level in range(layer_total):
        near = halo(hidden, 1)
        far = halo(hidden, 2)
        parts = [far, near, hidden, swap(near), swap(far)]
        hidden = run_layer(band, parts, degree_f, weights_all, level, block_size)
        outputs.append(hidden)

    stacked = jnp.stack(outputs)
    arrived = []
    for shift in range(0, section_count, group):
        sending = lax.dynamic_index_in_dim(
            stacked, (section_index + shift) % section_count, 0, keepdims=False
        )
        if shift == 0:
            arrived.append(sending)
        else:
            pairs = [(s, (s + shift) % section_count) for s in range(section_count)]
            arrived.append(lax.ppermute(sending, "section", pairs))
    arrived = jnp.stack(arrived)
    chip = section_index // group
    gathered = [
        lax.dynamic_index_in_dim(arrived, (chip - m) % batch_total, 0, keepdims=False)
        for m in range(batch_total)
    ]
    return jnp.stack(gathered)[None]


def solution(mesh):
    return jax.shard_map(
        body,
        mesh=mesh,
        in_specs=(
            P(None, "blk", None),
            P(None, "blk", None, None),
            P(None, "blk"),
            P(None, "blk"),
            P(None, "blk"),
            P(None, "blk"),
            P("section", None, None),
            P("section", None, None),
        ),
        out_specs=P("section", None, "blk", None),
        check_vma=False,
    )
```

```python
import jax
import jax.numpy as jnp
from jax import lax
from jax.experimental import pallas as pl
from jax.experimental.pallas import tpu as pltpu
from jax.sharding import PartitionSpec as P

REACH = 2


def _band_kernel(rows_ref, cols_ref, count_ref, values_ref, band_ref):
    block = values_ref.shape[1]
    band_ref[...] = jnp.zeros(band_ref.shape, band_ref.dtype)

    def place(k, carry):
        r = pl.multiple_of(rows_ref[k] * block, block)
        c = pl.multiple_of(cols_ref[k] * block, block)
        band_ref[pl.ds(r, block), pl.ds(c, block)] = values_ref[k]
        return carry

    lax.fori_loop(0, count_ref[0], place, 0)


def build_band(row_local, column_local, count, values, rows_dev, band_cols):
    return pl.pallas_call(
        _band_kernel,
        out_shape=jax.ShapeDtypeStruct((rows_dev, band_cols), values.dtype),
        in_specs=[pl.BlockSpec(memory_space=pltpu.SMEM)] * 3
        + [pl.BlockSpec(memory_space=pltpu.VMEM)],
        out_specs=pl.BlockSpec(memory_space=pltpu.VMEM),
    )(row_local, column_local, count, values)


def _layer_kernel(band_ref, p0, p1, p2, p3, p4, own_ref, degree_ref, ws_ref, wn_ref, out_ref):
    rows = p2.shape[0]
    parts = (p0, p1, p2, p3, p4)
    summed = jnp.dot(
        band_ref[:, pl.ds(2 * rows, rows)], p2[...], preferred_element_type=jnp.float32
    )
    for position in (1, 3, 0, 4):
        summed = summed + jnp.dot(
            band_ref[:, pl.ds(position * rows, rows)],
            parts[position][...],
            preferred_element_type=jnp.float32,
        )
    neighbour_mean = (summed / degree_ref[...]).astype(jnp.bfloat16)
    combined = jnp.dot(own_ref[...], ws_ref[...], preferred_element_type=jnp.float32) + jnp.dot(
        neighbour_mean, wn_ref[...], preferred_element_type=jnp.float32
    )
    active = jnp.maximum(combined, 0.0)
    scale = lax.rsqrt(jnp.mean(active * active, axis=-1, keepdims=True) + 1e-05)
    out_ref[...] = (active * scale).astype(out_ref.dtype)


def run_layer(band, parts, degree_f, weights_all, level):
    rows, width = parts[2].shape
    band_cols = band.shape[1]
    tile = rows
    whole = pl.BlockSpec((rows, width), lambda i: (0, 0))
    return pl.pallas_call(
        _layer_kernel,
        out_shape=jax.ShapeDtypeStruct((rows, width), jnp.bfloat16),
        grid=(rows // tile,),
        in_specs=[
            pl.BlockSpec((tile, band_cols), lambda i: (i, 0)),
            whole,
            whole,
            whole,
            whole,
            whole,
            pl.BlockSpec((tile, width), lambda i: (i, 0)),
            pl.BlockSpec((tile, 1), lambda i: (i, 0)),
            pl.BlockSpec((None, None, width, width), lambda i: (level, 0, 0, 0)),
            pl.BlockSpec((None, None, width, width), lambda i: (level, 1, 0, 0)),
        ],
        out_specs=pl.BlockSpec((tile, width), lambda i: (i, 0)),
        cost_estimate=pl.CostEstimate(
            flops=2 * rows * band_cols * width + 4 * rows * width * width,
            bytes_accessed=band.size * 2 + 6 * rows * width * 2,
            transcendentals=rows,
        ),
    )(band, *parts, parts[2], degree_f, weights_all, weights_all)


def body(
    features, tile_values, tile_rows, tile_cols, tile_count, degrees, self_weight, neighbour_weight
):
    batch_total, rows_dev, feature_width = features.shape
    slot_total, block_size = tile_values.shape[1], tile_values.shape[2]
    blocks_dev = rows_dev // block_size
    window_span = 2 * REACH + 1
    band_width = window_span * blocks_dev
    blk_count = lax.axis_size("blk")
    section_count = lax.axis_size("section")
    layer_total = section_count
    blk_index = lax.axis_index("blk")
    section_index = lax.axis_index("section")

    weights_all = lax.all_gather(jnp.stack([self_weight[0], neighbour_weight[0]]), "section")

    group = section_count // batch_total
    batch = section_index // group
    odd = section_index % 2 == 1

    def halo(x, reach):
        pairs = []
        for s in range(section_count):
            by = reach if s % 2 == 1 else -reach
            for b in range(blk_count):
                pairs.append((s * blk_count + b, s * blk_count + (b + by) % blk_count))
        return lax.ppermute(x, ("section", "blk"), pairs)

    def swap(x):
        pairs = [(s, s ^ 1) for s in range(section_count)]
        return lax.ppermute(x, "section", pairs)

    values = lax.dynamic_index_in_dim(tile_values, batch, 0, keepdims=False)
    rows = lax.dynamic_index_in_dim(tile_rows, batch, 0, keepdims=False)
    cols = lax.dynamic_index_in_dim(tile_cols, batch, 0, keepdims=False)
    count = lax.dynamic_index_in_dim(tile_count, batch, 0, keepdims=False)[0]
    degree = lax.dynamic_index_in_dim(degrees, batch, 0, keepdims=False)
    hidden = lax.dynamic_index_in_dim(features, batch, 0, keepdims=False)

    column_dev = cols // blocks_dev
    shifted = jnp.mod(column_dev - blk_index + REACH, blk_count)
    shifted = jnp.where(odd, shifted, 2 * REACH - shifted)
    column_local = shifted * blocks_dev + jnp.mod(cols, blocks_dev)
    row_local = rows - blk_index * blocks_dev
    band = build_band(
        jnp.clip(row_local, 0, blocks_dev - 1),
        jnp.clip(column_local, 0, band_width - 1),
        jnp.clip(count, 0, slot_total).reshape(1),
        values,
        rows_dev,
        band_width * block_size,
    )
    degree_f = degree.astype(jnp.float32)[:, None]

    outputs = []
    for level in range(layer_total):
        near = halo(hidden, 1)
        far = halo(hidden, 2)
        parts = [far, near, hidden, swap(near), swap(far)]
        hidden = run_layer(band, parts, degree_f, weights_all, level)
        outputs.append(hidden)

    stacked = jnp.stack(outputs)
    arrived = []
    for shift in range(0, section_count, group):
        sending = lax.dynamic_index_in_dim(
            stacked, (section_index + shift) % section_count, 0, keepdims=False
        )
        if shift == 0:
            arrived.append(sending)
        else:
            pairs = [(s, (s + shift) % section_count) for s in range(section_count)]
            arrived.append(lax.ppermute(sending, "section", pairs))
    arrived = jnp.stack(arrived)
    chip = section_index // group
    gathered = [
        lax.dynamic_index_in_dim(arrived, (chip - m) % batch_total, 0, keepdims=False)
        for m in range(batch_total)
    ]
    return jnp.stack(gathered)[None]


def solution(mesh):
    return jax.shard_map(
        body,
        mesh=mesh,
        in_specs=(
            P(None, "blk", None),
            P(None, "blk", None, None),
            P(None, "blk"),
            P(None, "blk"),
            P(None, "blk"),
            P(None, "blk"),
            P("section", None, None),
            P("section", None, None),
        ),
        out_specs=P("section", None, "blk", None),
        check_vma=False,
    )
```

```python
import jax
import jax.numpy as jnp
from jax import lax
from jax.experimental import pallas as pl
from jax.experimental.pallas import tpu as pltpu
from jax.sharding import PartitionSpec as P

REACH = 2


def _band_kernel(rows_ref, cols_ref, count_ref, values_ref, band_ref):
    block = values_ref.shape[1]
    band_ref[...] = jnp.zeros(band_ref.shape, band_ref.dtype)

    def place(k, carry):
        r = pl.multiple_of(rows_ref[k] * block, block)
        c = pl.multiple_of(cols_ref[k] * block, block)
        band_ref[pl.ds(r, block), pl.ds(c, block)] = values_ref[k]
        return carry

    lax.fori_loop(0, count_ref[0], place, 0)


def build_band(row_local, column_local, count, values, rows_dev, band_cols):
    return pl.pallas_call(
        _band_kernel,
        out_shape=jax.ShapeDtypeStruct((rows_dev, band_cols), values.dtype),
        in_specs=[pl.BlockSpec(memory_space=pltpu.SMEM)] * 3
        + [pl.BlockSpec(memory_space=pltpu.VMEM)],
        out_specs=pl.BlockSpec(memory_space=pltpu.VMEM),
    )(row_local, column_local, count, values)


def _layer_kernel(band_ref, p0, p1, p2, p3, p4, own_ref, degree_ref, ws_ref, wn_ref, out_ref):
    rows = p2.shape[0]
    parts = (p0, p1, p2, p3, p4)
    summed = jnp.dot(
        band_ref[:, pl.ds(2 * rows, rows)], p2[...], preferred_element_type=jnp.float32
    )
    for position in (1, 3, 0, 4):
        summed = summed + jnp.dot(
            band_ref[:, pl.ds(position * rows, rows)],
            parts[position][...],
            preferred_element_type=jnp.float32,
        )
    neighbour_mean = (summed / degree_ref[...]).astype(jnp.bfloat16)
    combined = jnp.dot(own_ref[...], ws_ref[...], preferred_element_type=jnp.float32) + jnp.dot(
        neighbour_mean, wn_ref[...], preferred_element_type=jnp.float32
    )
    active = jnp.maximum(combined, 0.0)
    scale = lax.rsqrt(jnp.mean(active * active, axis=-1, keepdims=True) + 1e-05)
    out_ref[...] = (active * scale).astype(out_ref.dtype)


def run_layer(band, parts, degree_f, weights_all, level):
    rows, width = parts[2].shape
    band_cols = band.shape[1]
    tile = rows
    whole = pl.BlockSpec((rows, width), lambda i: (0, 0))
    return pl.pallas_call(
        _layer_kernel,
        out_shape=jax.ShapeDtypeStruct((rows, width), jnp.bfloat16),
        grid=(rows // tile,),
        in_specs=[
            pl.BlockSpec((tile, band_cols), lambda i: (i, 0)),
            whole,
            whole,
            whole,
            whole,
            whole,
            pl.BlockSpec((tile, width), lambda i: (i, 0)),
            pl.BlockSpec((tile, 1), lambda i: (i, 0)),
            pl.BlockSpec((None, None, width, width), lambda i: (level, 0, 0, 0)),
            pl.BlockSpec((None, None, width, width), lambda i: (level, 1, 0, 0)),
        ],
        out_specs=pl.BlockSpec((tile, width), lambda i: (i, 0)),
        cost_estimate=pl.CostEstimate(
            flops=2 * rows * band_cols * width + 4 * rows * width * width,
            bytes_accessed=band.size * 2 + 6 * rows * width * 2,
            transcendentals=rows,
        ),
    )(band, *parts, parts[2], degree_f, weights_all, weights_all)


def body(
    features, tile_values, tile_rows, tile_cols, tile_count, degrees, self_weight, neighbour_weight
):
    batch_total, rows_dev, feature_width = features.shape
    slot_total, block_size = tile_values.shape[1], tile_values.shape[2]
    blocks_dev = rows_dev // block_size
    window_span = 2 * REACH + 1
    band_width = window_span * blocks_dev
    blk_count = lax.axis_size("blk")
    section_count = lax.axis_size("section")
    layer_total = section_count
    blk_index = lax.axis_index("blk")
    section_index = lax.axis_index("section")

    weights_all = lax.all_gather(jnp.stack([self_weight[0], neighbour_weight[0]]), "section")

    group = section_count // batch_total
    batch = section_index // group
    odd = section_index % 2 == 1

    def halo(x, reach):
        pairs = []
        for s in range(section_count):
            by = reach if s % 2 == 1 else -reach
            for b in range(blk_count):
                pairs.append((s * blk_count + b, s * blk_count + (b + by) % blk_count))
        return lax.ppermute(x, ("section", "blk"), pairs)

    def swap(x):
        pairs = [(s, s ^ 1) for s in range(section_count)]
        return lax.ppermute(x, "section", pairs)

    values = lax.dynamic_index_in_dim(tile_values, batch, 0, keepdims=False)
    rows = lax.dynamic_index_in_dim(tile_rows, batch, 0, keepdims=False)
    cols = lax.dynamic_index_in_dim(tile_cols, batch, 0, keepdims=False)
    count = lax.dynamic_index_in_dim(tile_count, batch, 0, keepdims=False)[0]
    degree = lax.dynamic_index_in_dim(degrees, batch, 0, keepdims=False)
    hidden = lax.dynamic_index_in_dim(features, batch, 0, keepdims=False)

    column_dev = cols // blocks_dev
    shifted = jnp.mod(column_dev - blk_index + REACH, blk_count)
    shifted = jnp.where(odd, shifted, 2 * REACH - shifted)
    column_local = shifted * blocks_dev + jnp.mod(cols, blocks_dev)
    row_local = rows - blk_index * blocks_dev
    band = build_band(
        jnp.clip(row_local, 0, blocks_dev - 1),
        jnp.clip(column_local, 0, band_width - 1),
        jnp.clip(count, 0, slot_total).reshape(1),
        values,
        rows_dev,
        band_width * block_size,
    )
    degree_f = degree.astype(jnp.float32)[:, None]

    outputs = []
    for level in range(layer_total):
        near = halo(hidden, 1)
        far = halo(hidden, 2)
        parts = [far, near, hidden, swap(near), swap(far)]
        hidden = run_layer(band, parts, degree_f, weights_all, level)
        outputs.append(hidden)

    last = layer_total - 1

    def pick(levels, at):
        chosen = outputs[levels[0]]
        for level in levels[1:]:
            chosen = jnp.where(at == level, outputs[level], chosen)
        return chosen

    arrived = [pick(list(range(layer_total)), section_index)]
    for shift in range(group, section_count, group):
        at = (section_index + shift) % section_count
        early_pairs = [
            (s, (s + shift) % section_count)
            for s in range(section_count)
            if (s + shift) % section_count != last
        ]
        early = lax.ppermute(pick(list(range(last)), at), "section", early_pairs)
        late = lax.ppermute(outputs[last], "section", [((last - shift) % section_count, last)])
        arrived.append(jnp.where(section_index == last, late, early))
    chip = section_index // group
    gathered = []
    for m in range(batch_total):
        which = (chip - m) % batch_total
        chosen = arrived[0]
        for j in range(1, batch_total):
            chosen = jnp.where(which == j, arrived[j], chosen)
        gathered.append(chosen)
    return jnp.stack(gathered)[None]


def solution(mesh):
    return jax.shard_map(
        body,
        mesh=mesh,
        in_specs=(
            P(None, "blk", None),
            P(None, "blk", None, None),
            P(None, "blk"),
            P(None, "blk"),
            P(None, "blk"),
            P(None, "blk"),
            P("section", None, None),
            P("section", None, None),
        ),
        out_specs=P("section", None, "blk", None),
        check_vma=False,
    )
```

```python
import jax
import jax.numpy as jnp
from jax import lax
from jax.experimental import pallas as pl
from jax.experimental.pallas import tpu as pltpu
from jax.sharding import PartitionSpec as P

REACH = 2


def _band_kernel(rows_ref, cols_ref, count_ref, values_ref, band_ref):
    block = values_ref.shape[1]
    band_ref[...] = jnp.zeros(band_ref.shape, band_ref.dtype)

    def place(k, carry):
        r = pl.multiple_of(rows_ref[k] * block, block)
        c = pl.multiple_of(cols_ref[k] * block, block)
        band_ref[pl.ds(r, block), pl.ds(c, block)] = values_ref[k]
        return carry

    lax.fori_loop(0, count_ref[0], place, 0)


def build_band(row_local, column_local, count, values, rows_dev, band_cols):
    return pl.pallas_call(
        _band_kernel,
        out_shape=jax.ShapeDtypeStruct((rows_dev, band_cols), values.dtype),
        in_specs=[pl.BlockSpec(memory_space=pltpu.SMEM)] * 3
        + [pl.BlockSpec(memory_space=pltpu.VMEM)],
        out_specs=pl.BlockSpec(memory_space=pltpu.VMEM),
    )(row_local, column_local, count, values)


def _partial_kernel(band_ref, far_ref, near_ref, out_ref):
    rows = far_ref.shape[0]
    out_ref[...] = jnp.dot(
        band_ref[:, pl.ds(0, rows)], far_ref[...], preferred_element_type=jnp.float32
    ) + jnp.dot(band_ref[:, pl.ds(rows, rows)], near_ref[...], preferred_element_type=jnp.float32)


def side_part(band, far, near):
    rows, width = far.shape
    return pl.pallas_call(
        _partial_kernel,
        out_shape=jax.ShapeDtypeStruct((rows, width), jnp.float32),
        grid=(1,),
        in_specs=[
            pl.BlockSpec((rows, REACH * rows), lambda i: (0, 0)),
            pl.BlockSpec((rows, width), lambda i: (0, 0)),
            pl.BlockSpec((rows, width), lambda i: (0, 0)),
        ],
        out_specs=pl.BlockSpec((rows, width), lambda i: (0, 0)),
        cost_estimate=pl.CostEstimate(
            flops=4 * rows * rows * width,
            bytes_accessed=2 * rows * rows * 2 + 2 * rows * width * 2 + rows * width * 4,
            transcendentals=0,
        ),
    )(band, far, near)


def _layer_kernel(band_ref, own_ref, mine_ref, theirs_ref, degree_ref, ws_ref, wn_ref, out_ref):
    summed = (mine_ref[...] + theirs_ref[...]) + jnp.dot(
        band_ref[...], own_ref[...], preferred_element_type=jnp.float32
    )
    neighbour_mean = (summed / degree_ref[...]).astype(jnp.bfloat16)
    combined = jnp.dot(own_ref[...], ws_ref[...], preferred_element_type=jnp.float32) + jnp.dot(
        neighbour_mean, wn_ref[...], preferred_element_type=jnp.float32
    )
    active = jnp.maximum(combined, 0.0)
    scale = lax.rsqrt(jnp.mean(active * active, axis=-1, keepdims=True) + 1e-05)
    out_ref[...] = (active * scale).astype(out_ref.dtype)


def run_layer(band, own, mine, theirs, degree_f, weights_all, level):
    rows, width = own.shape
    whole = pl.BlockSpec((rows, width), lambda i: (0, 0))
    return pl.pallas_call(
        _layer_kernel,
        out_shape=jax.ShapeDtypeStruct((rows, width), jnp.bfloat16),
        grid=(1,),
        in_specs=[
            pl.BlockSpec((rows, rows), lambda i: (0, REACH)),
            whole,
            whole,
            whole,
            pl.BlockSpec((rows, 1), lambda i: (0, 0)),
            pl.BlockSpec((None, None, width, width), lambda i: (level, 0, 0, 0)),
            pl.BlockSpec((None, None, width, width), lambda i: (level, 1, 0, 0)),
        ],
        out_specs=whole,
        cost_estimate=pl.CostEstimate(
            flops=2 * rows * rows * width + 4 * rows * width * width,
            bytes_accessed=rows * rows * 2 + 2 * rows * width * 2 + 2 * rows * width * 4,
            transcendentals=rows,
        ),
    )(band, own, mine, theirs, degree_f, weights_all, weights_all)


def body(
    features, tile_values, tile_rows, tile_cols, tile_count, degrees, self_weight, neighbour_weight
):
    batch_total, rows_dev, feature_width = features.shape
    slot_total, block_size = tile_values.shape[1], tile_values.shape[2]
    blocks_dev = rows_dev // block_size
    window_span = 2 * REACH + 1
    band_width = window_span * blocks_dev
    blk_count = lax.axis_size("blk")
    section_count = lax.axis_size("section")
    layer_total = section_count
    blk_index = lax.axis_index("blk")
    section_index = lax.axis_index("section")

    weights_all = lax.all_gather(jnp.stack([self_weight[0], neighbour_weight[0]]), "section")

    group = section_count // batch_total
    batch = section_index // group
    odd = section_index % 2 == 1

    def halo(x, reach):
        pairs = []
        for s in range(section_count):
            by = reach if s % 2 == 1 else -reach
            for b in range(blk_count):
                pairs.append((s * blk_count + b, s * blk_count + (b + by) % blk_count))
        return lax.ppermute(x, ("section", "blk"), pairs)

    def swap(x):
        pairs = [(s, s ^ 1) for s in range(section_count)]
        return lax.ppermute(x, "section", pairs)

    values = lax.dynamic_index_in_dim(tile_values, batch, 0, keepdims=False)
    rows = lax.dynamic_index_in_dim(tile_rows, batch, 0, keepdims=False)
    cols = lax.dynamic_index_in_dim(tile_cols, batch, 0, keepdims=False)
    count = lax.dynamic_index_in_dim(tile_count, batch, 0, keepdims=False)[0]
    degree = lax.dynamic_index_in_dim(degrees, batch, 0, keepdims=False)
    hidden = lax.dynamic_index_in_dim(features, batch, 0, keepdims=False)

    column_dev = cols // blocks_dev
    shifted = jnp.mod(column_dev - blk_index + REACH, blk_count)
    shifted = jnp.where(odd, shifted, 2 * REACH - shifted)
    column_local = shifted * blocks_dev + jnp.mod(cols, blocks_dev)
    row_local = rows - blk_index * blocks_dev
    band = build_band(
        jnp.clip(row_local, 0, blocks_dev - 1),
        jnp.clip(column_local, 0, band_width - 1),
        jnp.clip(count, 0, slot_total).reshape(1),
        values,
        rows_dev,
        band_width * block_size,
    )
    degree_f = degree.astype(jnp.float32)[:, None]

    outputs = []
    for level in range(layer_total):
        near = halo(hidden, 1)
        far = halo(hidden, 2)
        mine = side_part(band, far, near)
        hidden = run_layer(band, hidden, mine, swap(mine), degree_f, weights_all, level)
        outputs.append(hidden)

    stacked = jnp.stack(outputs)
    arrived = []
    for shift in range(0, section_count, group):
        sending = lax.dynamic_index_in_dim(
            stacked, (section_index + shift) % section_count, 0, keepdims=False
        )
        if shift == 0:
            arrived.append(sending)
        else:
            pairs = [(s, (s + shift) % section_count) for s in range(section_count)]
            arrived.append(lax.ppermute(sending, "section", pairs))
    arrived = jnp.stack(arrived)
    chip = section_index // group
    gathered = [
        lax.dynamic_index_in_dim(arrived, (chip - m) % batch_total, 0, keepdims=False)
        for m in range(batch_total)
    ]
    return jnp.stack(gathered)[None]


def solution(mesh):
    return jax.shard_map(
        body,
        mesh=mesh,
        in_specs=(
            P(None, "blk", None),
            P(None, "blk", None, None),
            P(None, "blk"),
            P(None, "blk"),
            P(None, "blk"),
            P(None, "blk"),
            P("section", None, None),
            P("section", None, None),
        ),
        out_specs=P("section", None, "blk", None),
        check_vma=False,
    )
```

```python
import jax
import jax.numpy as jnp
from jax import lax
from jax.experimental import pallas as pl
from jax.experimental.pallas import tpu as pltpu
from jax.sharding import PartitionSpec as P

REACH = 2


def _band_kernel(rows_ref, cols_ref, count_ref, batch_ref, values_ref, band_ref):
    block = values_ref.shape[1]
    band_ref[...] = jnp.zeros(band_ref.shape, band_ref.dtype)

    def place(k, carry):
        r = pl.multiple_of(rows_ref[k] * block, block)
        c = pl.multiple_of(cols_ref[k] * block, block)
        band_ref[pl.ds(r, block), pl.ds(c, block)] = values_ref[k]
        return carry

    lax.fori_loop(0, count_ref[0], place, 0)


def build_band(row_local, column_local, count, batch, tile_values, rows_dev, band_cols):
    slots, block = tile_values.shape[1], tile_values.shape[2]
    return pl.pallas_call(
        _band_kernel,
        out_shape=jax.ShapeDtypeStruct((rows_dev, band_cols), tile_values.dtype),
        grid_spec=pltpu.PrefetchScalarGridSpec(
            num_scalar_prefetch=4,
            grid=(1,),
            in_specs=[
                pl.BlockSpec((None, slots, block, block), lambda i, r, c, n, b: (b[0], 0, 0, 0))
            ],
            out_specs=pl.BlockSpec((rows_dev, band_cols), lambda i, r, c, n, b: (0, 0)),
        ),
    )(row_local, column_local, count, batch, tile_values)


def _layer_kernel(band_ref, p0, p1, p2, p3, p4, degree_ref, ws_ref, wn_ref, out_ref):
    rows = p2.shape[0]
    parts = (p0, p1, p2, p3, p4)
    summed = jnp.dot(
        band_ref[:, pl.ds(2 * rows, rows)], p2[...], preferred_element_type=jnp.float32
    )
    for position in (1, 3, 0, 4):
        summed = summed + jnp.dot(
            band_ref[:, pl.ds(position * rows, rows)],
            parts[position][...],
            preferred_element_type=jnp.float32,
        )
    neighbour_mean = (summed / degree_ref[...]).astype(jnp.bfloat16)
    combined = jnp.dot(p2[...], ws_ref[...], preferred_element_type=jnp.float32) + jnp.dot(
        neighbour_mean, wn_ref[...], preferred_element_type=jnp.float32
    )
    active = jnp.maximum(combined, 0.0)
    scale = lax.rsqrt(jnp.mean(active * active, axis=-1, keepdims=True) + 1e-05)
    out_ref[...] = (active * scale).astype(out_ref.dtype)


def run_layer(band, parts, degree_f, ws, wn):
    rows, width = parts[2].shape
    return pl.pallas_call(
        _layer_kernel,
        out_shape=jax.ShapeDtypeStruct((rows, width), jnp.bfloat16),
        in_specs=[pl.BlockSpec(memory_space=pltpu.VMEM)] * 9,
        out_specs=pl.BlockSpec(memory_space=pltpu.VMEM),
        cost_estimate=pl.CostEstimate(
            flops=2 * rows * band.shape[1] * width + 4 * rows * width * width,
            bytes_accessed=band.size * 2 + 6 * rows * width * 2,
            transcendentals=rows,
        ),
    )(band, *parts, degree_f, ws, wn)


def body(
    features, tile_values, tile_rows, tile_cols, tile_count, degrees, self_weight, neighbour_weight
):
    batch_total, rows_dev, feature_width = features.shape
    slot_total, block_size = tile_values.shape[1], tile_values.shape[2]
    blocks_dev = rows_dev // block_size
    window_span = 2 * REACH + 1
    band_width = window_span * blocks_dev
    blk_count = lax.axis_size("blk")
    section_count = lax.axis_size("section")
    layer_total = section_count
    blk_index = lax.axis_index("blk")
    section_index = lax.axis_index("section")

    weights_all = lax.all_gather(jnp.stack([self_weight[0], neighbour_weight[0]]), "section")
    self_all = weights_all[:, 0]
    neighbour_all = weights_all[:, 1]

    group = section_count // batch_total
    batch = section_index // group
    odd = section_index % 2 == 1

    def halo(x, reach):
        pairs = []
        for s in range(section_count):
            by = reach if s % 2 == 1 else -reach
            for b in range(blk_count):
                pairs.append((s * blk_count + b, s * blk_count + (b + by) % blk_count))
        return lax.ppermute(x, ("section", "blk"), pairs)

    def swap(x):
        pairs = [(s, s ^ 1) for s in range(section_count)]
        return lax.ppermute(x, "section", pairs)

    rows = lax.dynamic_index_in_dim(tile_rows, batch, 0, keepdims=False)
    cols = lax.dynamic_index_in_dim(tile_cols, batch, 0, keepdims=False)
    count = lax.dynamic_index_in_dim(tile_count, batch, 0, keepdims=False)[0]
    degree = lax.dynamic_index_in_dim(degrees, batch, 0, keepdims=False)
    hidden = lax.dynamic_index_in_dim(features, batch, 0, keepdims=False)

    column_dev = cols // blocks_dev
    shifted = jnp.mod(column_dev - blk_index + REACH, blk_count)
    shifted = jnp.where(odd, shifted, 2 * REACH - shifted)
    column_local = shifted * blocks_dev + jnp.mod(cols, blocks_dev)
    row_local = rows - blk_index * blocks_dev
    band = build_band(
        jnp.clip(row_local, 0, blocks_dev - 1),
        jnp.clip(column_local, 0, band_width - 1),
        jnp.clip(count, 0, slot_total).reshape(1),
        jnp.clip(batch, 0, batch_total - 1).astype(jnp.int32).reshape(1),
        tile_values,
        rows_dev,
        band_width * block_size,
    )
    degree_f = degree.astype(jnp.float32)[:, None]

    outputs = []
    for level in range(layer_total):
        near = halo(hidden, 1)
        far = halo(hidden, 2)
        theirs = swap(jnp.concatenate([near, far], axis=0))
        parts = [far, near, hidden, theirs[:rows_dev], theirs[rows_dev:]]
        hidden = run_layer(band, parts, degree_f, self_all[level], neighbour_all[level])
        outputs.append(hidden)

    stacked = jnp.stack(outputs)
    arrived = []
    for shift in range(0, section_count, group):
        sending = lax.dynamic_index_in_dim(
            stacked, (section_index + shift) % section_count, 0, keepdims=False
        )
        if shift == 0:
            arrived.append(sending)
        else:
            pairs = [(s, (s + shift) % section_count) for s in range(section_count)]
            arrived.append(lax.ppermute(sending, "section", pairs))
    arrived = jnp.stack(arrived)
    chip = section_index // group
    gathered = [
        lax.dynamic_index_in_dim(arrived, (chip - m) % batch_total, 0, keepdims=False)
        for m in range(batch_total)
    ]
    return jnp.stack(gathered)[None]


def solution(mesh):
    return jax.shard_map(
        body,
        mesh=mesh,
        in_specs=(
            P(None, "blk", None),
            P(None, "blk", None, None),
            P(None, "blk"),
            P(None, "blk"),
            P(None, "blk"),
            P(None, "blk"),
            P("section", None, None),
            P("section", None, None),
        ),
        out_specs=P("section", None, "blk", None),
        check_vma=False,
    )
```

```python
import jax
import jax.numpy as jnp
from jax import lax
from jax.experimental import pallas as pl
from jax.experimental.pallas import tpu as pltpu
from jax.sharding import PartitionSpec as P

REACH = 2


def _band_kernel(rows_ref, cols_ref, count_ref, batch_ref, values_ref, band_ref):
    block = values_ref.shape[1]
    band_ref[...] = jnp.zeros(band_ref.shape, band_ref.dtype)

    def place(k, carry):
        r = pl.multiple_of(rows_ref[k] * block, block)
        c = pl.multiple_of(cols_ref[k] * block, block)
        band_ref[pl.ds(r, block), pl.ds(c, block)] = values_ref[k]
        return carry

    lax.fori_loop(0, count_ref[0], place, 0)


def build_band(row_local, column_local, count, batch, tile_values, rows_dev, band_cols):
    slots, block = tile_values.shape[1], tile_values.shape[2]
    return pl.pallas_call(
        _band_kernel,
        out_shape=jax.ShapeDtypeStruct((rows_dev, band_cols), tile_values.dtype),
        grid_spec=pltpu.PrefetchScalarGridSpec(
            num_scalar_prefetch=4,
            grid=(1,),
            in_specs=[
                pl.BlockSpec((None, slots, block, block), lambda i, r, c, n, b: (b[0], 0, 0, 0))
            ],
            out_specs=pl.BlockSpec((rows_dev, band_cols), lambda i, r, c, n, b: (0, 0)),
        ),
    )(row_local, column_local, count, batch, tile_values)


def _layer_kernel(band_ref, p0, p1, p2, p3, p4, degree_ref, ws_ref, wn_ref, out_ref):
    rows = p2.shape[0]
    parts = (p0, p1, p2, p3, p4)
    summed = jnp.dot(
        band_ref[:, pl.ds(2 * rows, rows)], p2[...], preferred_element_type=jnp.float32
    )
    for position in (1, 3, 0, 4):
        summed = summed + jnp.dot(
            band_ref[:, pl.ds(position * rows, rows)],
            parts[position][...],
            preferred_element_type=jnp.float32,
        )
    neighbour_mean = (summed / degree_ref[...]).astype(jnp.bfloat16)
    combined = jnp.dot(p2[...], ws_ref[...], preferred_element_type=jnp.float32) + jnp.dot(
        neighbour_mean, wn_ref[...], preferred_element_type=jnp.float32
    )
    active = jnp.maximum(combined, 0.0)
    scale = lax.rsqrt(jnp.mean(active * active, axis=-1, keepdims=True) + 1e-05)
    out_ref[...] = (active * scale).astype(out_ref.dtype)


def run_layer(band, parts, degree_f, ws, wn):
    rows, width = parts[2].shape
    return pl.pallas_call(
        _layer_kernel,
        out_shape=jax.ShapeDtypeStruct((rows, width), jnp.bfloat16),
        in_specs=[pl.BlockSpec(memory_space=pltpu.VMEM)] * 9,
        out_specs=pl.BlockSpec(memory_space=pltpu.VMEM),
        cost_estimate=pl.CostEstimate(
            flops=2 * rows * band.shape[1] * width + 4 * rows * width * width,
            bytes_accessed=band.size * 2 + 6 * rows * width * 2,
            transcendentals=rows,
        ),
    )(band, *parts, degree_f, ws, wn)


def _sum_kernel(band_ref, p0, p1, p2, p3, p4, out_ref):
    rows = p2.shape[0]
    parts = (p0, p1, p2, p3, p4)
    summed = jnp.dot(
        band_ref[:, pl.ds(2 * rows, rows)], p2[...], preferred_element_type=jnp.float32
    )
    for position in (1, 3, 0, 4):
        summed = summed + jnp.dot(
            band_ref[:, pl.ds(position * rows, rows)],
            parts[position][...],
            preferred_element_type=jnp.float32,
        )
    out_ref[...] = summed


def _combine_kernel(summed_ref, own_ref, degree_ref, ws_ref, wn_ref, out_ref):
    neighbour_mean = (summed_ref[...] / degree_ref[...]).astype(jnp.bfloat16)
    combined = jnp.dot(own_ref[...], ws_ref[...], preferred_element_type=jnp.float32) + jnp.dot(
        neighbour_mean, wn_ref[...], preferred_element_type=jnp.float32
    )
    active = jnp.maximum(combined, 0.0)
    scale = lax.rsqrt(jnp.mean(active * active, axis=-1, keepdims=True) + 1e-05)
    out_ref[...] = (active * scale).astype(out_ref.dtype)


def run_layer_split(band, parts, degree_f, ws, wn):
    rows, width = parts[2].shape
    vmem = pl.BlockSpec(memory_space=pltpu.VMEM)
    summed = pl.pallas_call(
        _sum_kernel,
        out_shape=jax.ShapeDtypeStruct((rows, width), jnp.float32),
        in_specs=[vmem] * 6,
        out_specs=vmem,
    )(band, *parts)
    return pl.pallas_call(
        _combine_kernel,
        out_shape=jax.ShapeDtypeStruct((rows, width), jnp.bfloat16),
        in_specs=[vmem] * 5,
        out_specs=vmem,
    )(summed, parts[2], degree_f, ws, wn)


def body(
    features, tile_values, tile_rows, tile_cols, tile_count, degrees, self_weight, neighbour_weight
):
    batch_total, rows_dev, feature_width = features.shape
    slot_total, block_size = tile_values.shape[1], tile_values.shape[2]
    blocks_dev = rows_dev // block_size
    window_span = 2 * REACH + 1
    band_width = window_span * blocks_dev
    blk_count = lax.axis_size("blk")
    section_count = lax.axis_size("section")
    layer_total = section_count
    blk_index = lax.axis_index("blk")
    section_index = lax.axis_index("section")

    weights_all = lax.all_gather(jnp.stack([self_weight[0], neighbour_weight[0]]), "section")
    self_all = weights_all[:, 0]
    neighbour_all = weights_all[:, 1]

    group = section_count // batch_total
    batch = section_index // group
    odd = section_index % 2 == 1

    def halo(x, reach):
        pairs = []
        for s in range(section_count):
            by = reach if s % 2 == 1 else -reach
            for b in range(blk_count):
                pairs.append((s * blk_count + b, s * blk_count + (b + by) % blk_count))
        return lax.ppermute(x, ("section", "blk"), pairs)

    def swap(x):
        pairs = [(s, s ^ 1) for s in range(section_count)]
        return lax.ppermute(x, "section", pairs)

    rows = lax.dynamic_index_in_dim(tile_rows, batch, 0, keepdims=False)
    cols = lax.dynamic_index_in_dim(tile_cols, batch, 0, keepdims=False)
    count = lax.dynamic_index_in_dim(tile_count, batch, 0, keepdims=False)[0]
    degree = lax.dynamic_index_in_dim(degrees, batch, 0, keepdims=False)
    hidden = lax.dynamic_index_in_dim(features, batch, 0, keepdims=False)

    column_dev = cols // blocks_dev
    shifted = jnp.mod(column_dev - blk_index + REACH, blk_count)
    shifted = jnp.where(odd, shifted, 2 * REACH - shifted)
    column_local = shifted * blocks_dev + jnp.mod(cols, blocks_dev)
    row_local = rows - blk_index * blocks_dev
    band = build_band(
        jnp.clip(row_local, 0, blocks_dev - 1),
        jnp.clip(column_local, 0, band_width - 1),
        jnp.clip(count, 0, slot_total).reshape(1),
        jnp.clip(batch, 0, batch_total - 1).astype(jnp.int32).reshape(1),
        tile_values,
        rows_dev,
        band_width * block_size,
    )
    degree_f = degree.astype(jnp.float32)[:, None]

    outputs = []
    for level in range(layer_total):
        near = halo(hidden, 1)
        far = halo(hidden, 2)
        theirs = swap(jnp.concatenate([near, far], axis=0))
        parts = [far, near, hidden, theirs[:rows_dev], theirs[rows_dev:]]
        layer_fn = run_layer_split if level == 0 else run_layer
        hidden = layer_fn(band, parts, degree_f, self_all[level], neighbour_all[level])
        outputs.append(hidden)

    stacked = jnp.stack(outputs)
    arrived = []
    for shift in range(0, section_count, group):
        sending = lax.dynamic_index_in_dim(
            stacked, (section_index + shift) % section_count, 0, keepdims=False
        )
        if shift == 0:
            arrived.append(sending)
        else:
            pairs = [(s, (s + shift) % section_count) for s in range(section_count)]
            arrived.append(lax.ppermute(sending, "section", pairs))
    arrived = jnp.stack(arrived)
    chip = section_index // group
    gathered = [
        lax.dynamic_index_in_dim(arrived, (chip - m) % batch_total, 0, keepdims=False)
        for m in range(batch_total)
    ]
    return jnp.stack(gathered)[None]


def solution(mesh):
    return jax.shard_map(
        body,
        mesh=mesh,
        in_specs=(
            P(None, "blk", None),
            P(None, "blk", None, None),
            P(None, "blk"),
            P(None, "blk"),
            P(None, "blk"),
            P(None, "blk"),
            P("section", None, None),
            P("section", None, None),
        ),
        out_specs=P("section", None, "blk", None),
        check_vma=False,
    )
```

```python
import jax
import jax.numpy as jnp
from jax import lax
from jax.experimental import pallas as pl
from jax.experimental.pallas import tpu as pltpu
from jax.sharding import PartitionSpec as P

REACH = 2


def _band_kernel(rows_ref, cols_ref, count_ref, batch_ref, values_ref, band_ref):
    block = values_ref.shape[1]
    band_ref[...] = jnp.zeros(band_ref.shape, band_ref.dtype)

    def place(k, carry):
        r = pl.multiple_of(rows_ref[k] * block, block)
        c = pl.multiple_of(cols_ref[k] * block, block)
        band_ref[pl.ds(r, block), pl.ds(c, block)] = values_ref[k]
        return carry

    lax.fori_loop(0, count_ref[0], place, 0)


def build_band(row_local, column_local, count, batch, tile_values, rows_dev, band_cols):
    slots, block = tile_values.shape[1], tile_values.shape[2]
    return pl.pallas_call(
        _band_kernel,
        out_shape=jax.ShapeDtypeStruct((rows_dev, band_cols), tile_values.dtype),
        grid_spec=pltpu.PrefetchScalarGridSpec(
            num_scalar_prefetch=4,
            grid=(1,),
            in_specs=[
                pl.BlockSpec((None, slots, block, block), lambda i, r, c, n, b: (b[0], 0, 0, 0))
            ],
            out_specs=pl.BlockSpec((rows_dev, band_cols), lambda i, r, c, n, b: (0, 0)),
        ),
    )(row_local, column_local, count, batch, tile_values)


def _layer_kernel(band_ref, p0, p1, p2, p3, p4, degree_ref, ws_ref, wn_ref, out_ref):
    rows = p2.shape[0]
    parts = (p0, p1, p2, p3, p4)
    summed = jnp.dot(
        band_ref[:, pl.ds(2 * rows, rows)], p2[...], preferred_element_type=jnp.float32
    )
    for position in (1, 3, 0, 4):
        summed = summed + jnp.dot(
            band_ref[:, pl.ds(position * rows, rows)],
            parts[position][...],
            preferred_element_type=jnp.float32,
        )
    neighbour_mean = (summed / degree_ref[...]).astype(jnp.bfloat16)
    combined = jnp.dot(p2[...], ws_ref[...], preferred_element_type=jnp.float32) + jnp.dot(
        neighbour_mean, wn_ref[...], preferred_element_type=jnp.float32
    )
    active = jnp.maximum(combined, 0.0)
    scale = lax.rsqrt(jnp.mean(active * active, axis=-1, keepdims=True) + 1e-05)
    out_ref[...] = (active * scale).astype(out_ref.dtype)


def weight_specs(level, width):
    return [
        pl.BlockSpec((None, None, width, width), lambda i: (level, 0, 0, 0)),
        pl.BlockSpec((None, None, width, width), lambda i: (level, 1, 0, 0)),
    ]


def whole_spec(shape):
    return pl.BlockSpec(shape, lambda i: (0,) * len(shape))


def run_layer(band, parts, degree_f, weights_all, level):
    rows, width = parts[2].shape
    return pl.pallas_call(
        _layer_kernel,
        out_shape=jax.ShapeDtypeStruct((rows, width), jnp.bfloat16),
        grid=(1,),
        in_specs=[whole_spec(band.shape)]
        + [whole_spec((rows, width))] * 5
        + [whole_spec(degree_f.shape)]
        + weight_specs(level, width),
        out_specs=whole_spec((rows, width)),
        cost_estimate=pl.CostEstimate(
            flops=2 * rows * band.shape[1] * width + 4 * rows * width * width,
            bytes_accessed=band.size * 2 + 6 * rows * width * 2,
            transcendentals=rows,
        ),
    )(band, *parts, degree_f, weights_all, weights_all)


def _sum_kernel(band_ref, p0, p1, p2, p3, p4, out_ref):
    rows = p2.shape[0]
    parts = (p0, p1, p2, p3, p4)
    summed = jnp.dot(
        band_ref[:, pl.ds(2 * rows, rows)], p2[...], preferred_element_type=jnp.float32
    )
    for position in (1, 3, 0, 4):
        summed = summed + jnp.dot(
            band_ref[:, pl.ds(position * rows, rows)],
            parts[position][...],
            preferred_element_type=jnp.float32,
        )
    out_ref[...] = summed


def _combine_kernel(summed_ref, own_ref, degree_ref, ws_ref, wn_ref, out_ref):
    neighbour_mean = (summed_ref[...] / degree_ref[...]).astype(jnp.bfloat16)
    combined = jnp.dot(own_ref[...], ws_ref[...], preferred_element_type=jnp.float32) + jnp.dot(
        neighbour_mean, wn_ref[...], preferred_element_type=jnp.float32
    )
    active = jnp.maximum(combined, 0.0)
    scale = lax.rsqrt(jnp.mean(active * active, axis=-1, keepdims=True) + 1e-05)
    out_ref[...] = (active * scale).astype(out_ref.dtype)


def run_layer_split(band, parts, degree_f, weights_all, level):
    rows, width = parts[2].shape
    vmem = pl.BlockSpec(memory_space=pltpu.VMEM)
    summed = pl.pallas_call(
        _sum_kernel,
        out_shape=jax.ShapeDtypeStruct((rows, width), jnp.float32),
        in_specs=[vmem] * 6,
        out_specs=vmem,
    )(band, *parts)
    return pl.pallas_call(
        _combine_kernel,
        out_shape=jax.ShapeDtypeStruct((rows, width), jnp.bfloat16),
        grid=(1,),
        in_specs=[whole_spec((rows, width))] * 2
        + [whole_spec(degree_f.shape)]
        + weight_specs(level, width),
        out_specs=whole_spec((rows, width)),
    )(summed, parts[2], degree_f, weights_all, weights_all)


def body(
    features, tile_values, tile_rows, tile_cols, tile_count, degrees, self_weight, neighbour_weight
):
    batch_total, rows_dev, feature_width = features.shape
    slot_total, block_size = tile_values.shape[1], tile_values.shape[2]
    blocks_dev = rows_dev // block_size
    window_span = 2 * REACH + 1
    band_width = window_span * blocks_dev
    blk_count = lax.axis_size("blk")
    section_count = lax.axis_size("section")
    layer_total = section_count
    blk_index = lax.axis_index("blk")
    section_index = lax.axis_index("section")

    weights_all = lax.all_gather(jnp.stack([self_weight[0], neighbour_weight[0]]), "section")

    group = section_count // batch_total
    batch = section_index // group
    odd = section_index % 2 == 1

    def halo(x, reach):
        pairs = []
        for s in range(section_count):
            by = reach if s % 2 == 1 else -reach
            for b in range(blk_count):
                pairs.append((s * blk_count + b, s * blk_count + (b + by) % blk_count))
        return lax.ppermute(x, ("section", "blk"), pairs)

    def swap(x):
        pairs = [(s, s ^ 1) for s in range(section_count)]
        return lax.ppermute(x, "section", pairs)

    rows = lax.dynamic_index_in_dim(tile_rows, batch, 0, keepdims=False)
    cols = lax.dynamic_index_in_dim(tile_cols, batch, 0, keepdims=False)
    count = lax.dynamic_index_in_dim(tile_count, batch, 0, keepdims=False)[0]
    degree = lax.dynamic_index_in_dim(degrees, batch, 0, keepdims=False)
    hidden = lax.dynamic_index_in_dim(features, batch, 0, keepdims=False)

    column_dev = cols // blocks_dev
    shifted = jnp.mod(column_dev - blk_index + REACH, blk_count)
    shifted = jnp.where(odd, shifted, 2 * REACH - shifted)
    column_local = shifted * blocks_dev + jnp.mod(cols, blocks_dev)
    row_local = rows - blk_index * blocks_dev
    band = build_band(
        jnp.clip(row_local, 0, blocks_dev - 1),
        jnp.clip(column_local, 0, band_width - 1),
        jnp.clip(count, 0, slot_total).reshape(1),
        jnp.clip(batch, 0, batch_total - 1).astype(jnp.int32).reshape(1),
        tile_values,
        rows_dev,
        band_width * block_size,
    )
    degree_f = degree.astype(jnp.float32)[:, None]

    outputs = []
    for level in range(layer_total):
        near = halo(hidden, 1)
        far = halo(hidden, 2)
        theirs = swap(jnp.concatenate([near, far], axis=0))
        parts = [far, near, hidden, theirs[:rows_dev], theirs[rows_dev:]]
        layer_fn = run_layer_split if level == 0 else run_layer
        hidden = layer_fn(band, parts, degree_f, weights_all, level)
        outputs.append(hidden)

    stacked = jnp.stack(outputs)
    arrived = []
    for shift in range(0, section_count, group):
        sending = lax.dynamic_index_in_dim(
            stacked, (section_index + shift) % section_count, 0, keepdims=False
        )
        if shift == 0:
            arrived.append(sending)
        else:
            pairs = [(s, (s + shift) % section_count) for s in range(section_count)]
            arrived.append(lax.ppermute(sending, "section", pairs))
    arrived = jnp.stack(arrived)
    chip = section_index // group
    gathered = [
        lax.dynamic_index_in_dim(arrived, (chip - m) % batch_total, 0, keepdims=False)
        for m in range(batch_total)
    ]
    return jnp.stack(gathered)[None]


def solution(mesh):
    return jax.shard_map(
        body,
        mesh=mesh,
        in_specs=(
            P(None, "blk", None),
            P(None, "blk", None, None),
            P(None, "blk"),
            P(None, "blk"),
            P(None, "blk"),
            P(None, "blk"),
            P("section", None, None),
            P("section", None, None),
        ),
        out_specs=P("section", None, "blk", None),
        check_vma=False,
    )
```
